32 devices in a mesh: dp: 16 (over z, x, core), vocab: 2 (over y).
Axes of the slice: x: 2, y: 2, z: 4, core: 2. Of those that a mesh axis runs over, the one named last changes fastest.
Arguments:
- hidden: bfloat16 [2048, 8192], P('dp', 'vocab')
- rank_factor: bfloat16 [256, 8192], P(None, 'vocab'), may hold values from -0.0625 to 0.0625
- vocab_factor: bfloat16 [256, 77824], P('dp', 'vocab')
- lengths: int32 [2048], P('dp'), may hold values from 0 to 4096, as said below
- targets: int32 [2048], P('dp'), may hold values from 0 to 77823
- cotangent: bfloat16 [2048], P('dp'), may hold values from -96 to 96
- grammar: int32 [64, 22], P('dp', 'vocab'), may hold values from 0 to 1073741823, as said below
- assign: int32 [2048], P('dp'), may hold values from 0 to 127, as said below
Outputs:
- grad_hidden: bfloat16 [2048, 8192], P('dp', 'vocab')
- grad_factor: float32 [256, 8192], P('dp', 'vocab')
The draws below stay inside these ranges and needn't reach their ends.
Inputs may be any that keep to these rules, and one draw needn't show every extreme that they name: `lengths`: in each aligned block of 128 rows the rows with a length above 0 come first; in every draw one such block has all 128 rows above 0 and a row of length 4096. `grammar`: only bits 0 to 29 of a word are used. `assign`: each aligned block of 128 entries is a permutation of 0 to 127.
All inputs are finite; a program needn't handle non-finite values.
Results may differ from the reference program's by a relative error of at most 0.0085.
Values may be sent and summed in bfloat16 or wider, within the bound.
No kernel may reach another device: no remote copies, remote signals or barrier semaphores. Data moves between devices by JAX's collectives and lax.ppermute only.
A program may use at most 128 MiB of HBM per device.

```python
import math
import jax
import jax.numpy as jnp
from jax import lax

D = 8192
R = 256
V = 77824
ROW_DEV = 128
RB = 32
PREFIX_MAX = 4096
ROWS = 2048
SHARE = 8
TILES = 304
MW = 11
MASK_WORDS = 22
MBLK = 64
N_DP = 16
N_VOCAB = 2


def draw_hidden(key, part):
    scale_key, base_key = jax.random.split(key, 2)
    scales = jnp.exp(jax.random.uniform(scale_key, (ROWS, 1), jnp.float32, math.log(0.5), math.log(5.0)))
    base = jnp.clip(jax.random.normal(base_key, (ROWS, D), jnp.float32), -6.0, 6.0)
    return (base * scales).astype(jnp.bfloat16)


def draw_vocab_factor(key, part):
    base_key = jax.random.fold_in(key, 1)
    base = jnp.clip(jax.random.normal(base_key, (R, V), jnp.float32), -6.0, 6.0)
    return (0.12 * base).astype(jnp.bfloat16)


def draw_lengths(key, part):
    devices = ROWS // ROW_DEV
    shift_key, full_key, value_key = jax.random.split(key, 3)
    shifts = jax.random.randint(shift_key, (devices, 1), 0, 4)
    fullest = jax.random.randint(full_key, (), 0, devices)
    device_ids = jnp.arange(devices, dtype=jnp.int32)[:, None]
    slots = jnp.arange(ROW_DEV, dtype=jnp.int32)[None, :]
    reduced = jnp.right_shift(jnp.full((devices, 1), ROW_DEV, jnp.int32), shifts)
    live = jnp.where(device_ids == fullest, ROW_DEV, reduced)
    values = jax.random.randint(value_key, (devices, ROW_DEV), 1, PREFIX_MAX + 1)
    values = jnp.where((device_ids == fullest) & (slots == 0), PREFIX_MAX, values)
    return jnp.where(slots < live, values, 0).reshape(ROWS).astype(jnp.int32)


def draw_grammar(key, part):
    upper = 1073741823
    level_key, first_key, second_key, third_key = jax.random.split(key, 4)
    levels = jax.random.randint(level_key, (MBLK, 1), 0, 4)
    levels = jnp.where(jnp.arange(MBLK, dtype=jnp.int32)[:, None] == 0, 0, levels)
    word_first = jax.random.randint(first_key, (MBLK, MASK_WORDS), 0, upper + 1)
    word_second = jax.random.randint(second_key, (MBLK, MASK_WORDS), 0, upper + 1)
    word_third = jax.random.randint(third_key, (MBLK, MASK_WORDS), 0, upper + 1)
    words = jnp.where(levels >= 1, word_first, upper)
    words = words & jnp.where(levels >= 2, word_second, upper)
    words = words & jnp.where(levels >= 3, word_third, upper)
    return words.astype(jnp.int32)


def draw_assign(key, part):
    devices = ROWS // ROW_DEV
    keys = jax.random.split(key, devices)

    def shuffled(single):
        return jax.random.permutation(single, ROW_DEV)
    return jax.vmap(shuffled)(keys).reshape(ROWS).astype(jnp.int32)


def touch_ends(array, key, least, top_value):
    longest = array.shape.index(max(array.shape))
    spots = []
    for shift in (0, 1):
        where = [jax.random.randint(jax.random.fold_in(key, axis), (), 0, length) for axis, length in enumerate(array.shape)]
        where[longest] = (where[longest] + shift) % array.shape[longest]
        spots.append(tuple(where))
    return array.at[spots[0]].set(least).at[spots[1]].set(top_value)


def steps_of(own_key, dims, cuts, smallest, largest):
    loudness = 1.0
    for dim, blocks in cuts:
        heights = jax.random.uniform(jax.random.fold_in(jax.random.fold_in(own_key, 6), dim), (blocks,), jnp.float32, smallest / len(cuts), largest / len(cuts))
        loudness = loudness * jnp.repeat(jnp.exp(heights), dims[dim] // blocks).reshape((-1,) + (1,) * (len(dims) - 1 - dim))
    return loudness


def bell_draw(stream_key, extent, scale, most, cuts=(), kind=jnp.bfloat16):
    array = scale * jax.random.normal(stream_key, extent, jnp.float32)
    if cuts:
        array = array * steps_of(stream_key, extent, cuts, -0.22, 0.18)
    return jnp.clip(array, -most, most).astype(kind)


def setup_inputs(seed: int = 0) -> dict:
    seeds = jax.random.split(jax.random.key(seed), 9)
    return {
        "hidden": draw_hidden(jax.random.fold_in(seeds[8], 71), 0),
        "rank_factor": bell_draw(seeds[1], (R, D), D ** -0.5, 0.0625, ((1, 2),)),
        "vocab_factor": draw_vocab_factor(jax.random.fold_in(seeds[8], 71), 0),
        "lengths": draw_lengths(jax.random.fold_in(seeds[8], 71), 0),
        "targets": touch_ends(jax.random.randint(seeds[4], (ROWS,), 0, V), jax.random.fold_in(seeds[4], 1), 0, V - 1).astype(jnp.int32),
        "cotangent": bell_draw(seeds[5], (ROWS,), 16.0, 96.0, ((0, 16),)),
        "grammar": draw_grammar(jax.random.fold_in(seeds[8], 71), 0),
        "assign": draw_assign(jax.random.fold_in(seeds[8], 71), 0),
    }


far_below = -1.0e30


def tile_bits(words):
    count = words.shape[0]
    shaped = words.reshape(count, N_VOCAB, MW)
    shifts = jnp.arange(30, dtype=jnp.int32)
    bits = jnp.right_shift(shaped[:, :, :, None], shifts) & 1
    bits = bits.reshape(count, N_VOCAB, MW * 30)[:, :, :TILES]
    return bits.reshape(count, N_VOCAB * TILES)


def reference(hidden, rank_factor, vocab_factor, lengths, targets, cotangent, grammar, assign):
    columns = jnp.arange(V, dtype=jnp.int32)

    def one_device(running, pieces):
        hidden_rows, length_rows, target_rows, cotangent_rows, word_rows = pieces
        latent = jnp.dot(hidden_rows, rank_factor.T, preferred_element_type=jnp.float32).astype(jnp.bfloat16)
        logits = jnp.dot(latent, vocab_factor, preferred_element_type=jnp.float32)
        tile_on = jnp.repeat(tile_bits(word_rows), RB, axis=0)
        tile_on = jnp.repeat(tile_on, 128, axis=1)
        target_hit = columns[None, :] == target_rows[:, None]
        allowed = (tile_on == 1) | target_hit
        masked = jnp.where(allowed, logits, far_below)
        peak = jnp.max(masked, axis=1, keepdims=True)
        powers = jnp.where(allowed, jnp.exp(masked - peak), 0.0)
        row_probs = powers / jnp.sum(powers, axis=1, keepdims=True)
        weight = cotangent_rows.astype(jnp.float32) * lengths_as_float(length_rows) / PREFIX_MAX
        score_grad = (weight[:, None] * (row_probs - target_hit.astype(jnp.float32))).astype(jnp.bfloat16)
        rank_grad = jnp.dot(score_grad, vocab_factor.T, preferred_element_type=jnp.float32).astype(jnp.bfloat16)
        row_grad = jnp.dot(rank_grad, rank_factor, preferred_element_type=jnp.float32).astype(jnp.bfloat16)
        running = running + jnp.dot(rank_grad.T, hidden_rows, preferred_element_type=jnp.float32)
        return running, row_grad

    pieces = (hidden.reshape(N_DP, ROW_DEV, D), lengths.reshape(N_DP, ROW_DEV), targets.reshape(N_DP, ROW_DEV),
              cotangent.reshape(N_DP, ROW_DEV), grammar.reshape(N_DP, ROW_DEV // RB, MASK_WORDS))
    grad_factor, row_grads = lax.scan(one_device, jnp.zeros((R, D), jnp.float32), pieces)
    order = assign.reshape(N_DP, ROW_DEV)

    def pick(grads_one, order_one):
        return jnp.take(grads_one, order_one, axis=0)

    picked = jax.vmap(pick)(row_grads, order)
    grad_hidden = picked.reshape(N_DP, N_DP, SHARE, D).transpose(1, 0, 2, 3).reshape(ROWS, D)
    return grad_hidden, grad_factor


def lengths_as_float(length_rows):
    return length_rows.astype(jnp.float32)
```

```python
import jax
import jax.numpy as jnp
from jax import lax
from jax.sharding import PartitionSpec as P

PREFIX_MAX = 4096
TILE = 128
WORD_BITS = 30


far_below = -1e30


def body(hidden, rank_factor, vocab_factor, lengths, targets, cotangent, grammar, assign):
    row_count = hidden.shape[0]
    rank = rank_factor.shape[0]
    groups = lax.axis_size("dp")
    share = row_count // groups
    width = vocab_factor.shape[1]
    cols = width // groups
    dp_index = lax.axis_index("dp")
    vocab_index = lax.axis_index("vocab")

    partial_latent = lax.dot_general(
        hidden, rank_factor, (((1,), (1,)), ((), ())), preferred_element_type=jnp.float32
    )
    latent = lax.psum(partial_latent, "vocab").astype(jnp.bfloat16)
    weight = cotangent.astype(jnp.float32) * lengths.astype(jnp.float32) / PREFIX_MAX

    latent_all = lax.all_gather(latent, "dp", axis=0, tiled=True)
    weight_all = lax.all_gather(weight, "dp", axis=0, tiled=True)
    target_all = lax.all_gather(targets, "dp", axis=0, tiled=True)
    words_all = lax.all_gather(grammar, "dp", axis=0, tiled=True)
    factor = lax.all_to_all(vocab_factor, "dp", split_axis=1, concat_axis=0, tiled=True)

    total_rows = latent_all.shape[0]
    row_block = total_rows // words_all.shape[0]
    first_col = dp_index * cols
    col_ids = first_col + jnp.arange(cols, dtype=jnp.int32)
    tile_ids = col_ids // TILE
    words = jnp.take(words_all, tile_ids // WORD_BITS, axis=1)
    block_on = (jnp.right_shift(words, (tile_ids % WORD_BITS)[None, :]) & 1) == 1
    tile_on = jnp.broadcast_to(block_on[:, None, :], (words_all.shape[0], row_block, cols)).reshape(
        total_rows, cols
    )
    target_local = target_all - vocab_index * width - first_col
    target_hit = jnp.arange(cols, dtype=jnp.int32)[None, :] == target_local[:, None]
    allowed = tile_on | target_hit

    logits = jnp.dot(latent_all, factor, preferred_element_type=jnp.float32)
    masked = jnp.where(allowed, logits, far_below)
    local_peak = jnp.max(masked, axis=1)
    local_total = jnp.sum(jnp.where(allowed, jnp.exp(masked - local_peak[:, None]), 0.0), axis=1)
    stats = lax.all_gather(jnp.stack([local_peak, local_total]), ("dp", "vocab"), axis=0)
    peak = jnp.max(stats[:, 0], axis=0)
    total = jnp.sum(stats[:, 1] * jnp.exp(stats[:, 0] - peak[None, :]), axis=0)

    powers = jnp.where(allowed, jnp.exp(masked - peak[:, None]), 0.0)
    row_probs = powers / total[:, None]
    score_grad = (weight_all[:, None] * (row_probs - target_hit.astype(jnp.float32))).astype(jnp.bfloat16)
    rank_partial = lax.dot_general(
        score_grad, factor, (((1,), (1,)), ((), ())), preferred_element_type=jnp.float32
    )
    rank_rows = lax.psum_scatter(rank_partial, "dp", scatter_dimension=0, tiled=True)
    rank_grad = lax.psum(rank_rows, "vocab").astype(jnp.bfloat16)

    grad_factor = lax.psum_scatter(
        lax.dot_general(
            rank_grad, hidden, (((0,), (0,)), ((), ())), preferred_element_type=jnp.float32
        ),
        "dp",
        scatter_dimension=0,
        tiled=True,
    )
    picked = jnp.take(rank_grad, assign, axis=0).reshape(groups, share, rank)
    slot_rank = lax.all_to_all(picked, "dp", split_axis=0, concat_axis=0, tiled=True).reshape(
        row_count, rank
    )
    grad_hidden = jnp.dot(slot_rank, rank_factor, preferred_element_type=jnp.float32).astype(
        jnp.bfloat16
    )
    return (grad_hidden, grad_factor)


def solution(mesh):
    return jax.shard_map(
        body,
        mesh=mesh,
        in_specs=(
            P("dp", "vocab"),
            P(None, "vocab"),
            P("dp", "vocab"),
            P("dp"),
            P("dp"),
            P("dp"),
            P("dp", "vocab"),
            P("dp"),
        ),
        out_specs=(P("dp", "vocab"), P("dp", "vocab")),
        check_vma=False,
    )
```

```python
import jax
import jax.numpy as jnp
from jax import lax
from jax.sharding import PartitionSpec as P

PREFIX_MAX = 4096
TILE = 128
WORD_BITS = 30


far_below = -1e30


def body(hidden, rank_factor, vocab_factor, lengths, targets, cotangent, grammar, assign):
    row_count = hidden.shape[0]
    rank = rank_factor.shape[0]
    groups = lax.axis_size("dp")
    share = row_count // groups
    width = vocab_factor.shape[1]
    cols = width // groups
    dp_index = lax.axis_index("dp")
    vocab_index = lax.axis_index("vocab")

    partial_latent = lax.dot_general(
        hidden, rank_factor, (((1,), (1,)), ((), ())), preferred_element_type=jnp.float32
    )
    latent = lax.psum(partial_latent, "vocab").astype(jnp.bfloat16)
    weight = cotangent.astype(jnp.float32) * lengths.astype(jnp.float32) / PREFIX_MAX

    words_local = grammar.shape[0]
    row_block = row_count // words_local
    mask_words = grammar.shape[1]
    row_words = jnp.repeat(grammar, row_block, axis=0)
    packed = jnp.concatenate(
        [
            latent.astype(jnp.float32),
            weight[:, None],
            targets.astype(jnp.float32)[:, None],
            jnp.right_shift(row_words, 15).astype(jnp.float32),
            (row_words & 32767).astype(jnp.float32),
        ],
        axis=1,
    )
    packed_all = lax.all_gather(packed, "dp", axis=0, tiled=True)
    factor = lax.all_to_all(vocab_factor, "dp", split_axis=1, concat_axis=0, tiled=True)

    total_rows = packed_all.shape[0]
    blocks = total_rows // row_block
    latent_all = packed_all[:, :rank].astype(jnp.bfloat16)
    weight_all = packed_all[:, rank]
    target_all = packed_all[:, rank + 1].astype(jnp.int32)
    block_rows = packed_all.reshape(blocks, row_block, -1)[:, 0, rank + 2 :].astype(jnp.int32)
    words_all = jnp.left_shift(block_rows[:, :mask_words], 15) | block_rows[:, mask_words:]

    first_col = dp_index * cols
    col_ids = first_col + jnp.arange(cols, dtype=jnp.int32)
    tile_ids = col_ids // TILE
    word_ids = tile_ids // WORD_BITS
    words = jnp.zeros((blocks, cols), jnp.int32)
    for w in range(mask_words):
        words = jnp.where(word_ids[None, :] == w, words_all[:, w : w + 1], words)
    block_on = (jnp.right_shift(words, (tile_ids % WORD_BITS)[None, :]) & 1) == 1
    tile_on = jnp.broadcast_to(block_on[:, None, :], (blocks, row_block, cols)).reshape(
        total_rows, cols
    )
    target_local = target_all - vocab_index * width - first_col
    target_hit = jnp.arange(cols, dtype=jnp.int32)[None, :] == target_local[:, None]
    allowed = tile_on | target_hit

    logits = jnp.dot(latent_all, factor, preferred_element_type=jnp.float32)
    masked = jnp.where(allowed, logits, far_below)
    peak = lax.pmax(jnp.max(masked, axis=1), ("dp", "vocab"))
    powers = jnp.where(allowed, jnp.exp(masked - peak[:, None]), 0.0)
    total = lax.psum(jnp.sum(powers, axis=1), ("dp", "vocab"))
    row_probs = powers / total[:, None]
    score_grad = (weight_all[:, None] * (row_probs - target_hit.astype(jnp.float32))).astype(jnp.bfloat16)
    rank_partial = lax.dot_general(
        score_grad, factor, (((1,), (1,)), ((), ())), preferred_element_type=jnp.float32
    )
    rank_rows = lax.psum_scatter(rank_partial, "dp", scatter_dimension=0, tiled=True)
    rank_grad = lax.psum(rank_rows, "vocab").astype(jnp.bfloat16)

    grad_factor = lax.psum_scatter(
        lax.dot_general(
            rank_grad, hidden, (((0,), (0,)), ((), ())), preferred_element_type=jnp.float32
        ),
        "dp",
        scatter_dimension=0,
        tiled=True,
    )
    picked = jnp.take(rank_grad, assign, axis=0).reshape(groups, share, rank)
    slot_rank = lax.all_to_all(picked, "dp", split_axis=0, concat_axis=0, tiled=True).reshape(
        row_count, rank
    )
    grad_hidden = jnp.dot(slot_rank, rank_factor, preferred_element_type=jnp.float32).astype(
        jnp.bfloat16
    )
    return (grad_hidden, grad_factor)


def solution(mesh):
    return jax.shard_map(
        body,
        mesh=mesh,
        in_specs=(
            P("dp", "vocab"),
            P(None, "vocab"),
            P("dp", "vocab"),
            P("dp"),
            P("dp"),
            P("dp"),
            P("dp", "vocab"),
            P("dp"),
        ),
        out_specs=(P("dp", "vocab"), P("dp", "vocab")),
        check_vma=False,
    )
```

```python
import jax
import jax.numpy as jnp
from jax import lax
from jax.sharding import PartitionSpec as P

PREFIX_MAX = 4096
TILE = 128
WORD_BITS = 30
CHUNKS = 4


far_below = -1e30


def chunk_count(tiles):
    for count in (CHUNKS, 2, 1):
        if tiles % count == 0:
            return count
    return 1


def body(hidden, rank_factor, vocab_factor, lengths, targets, cotangent, grammar, assign):
    row_count = hidden.shape[0]
    rank = rank_factor.shape[0]
    groups = lax.axis_size("dp")
    share = row_count // groups
    width = vocab_factor.shape[1]
    tiles = width // TILE
    chunks = chunk_count(tiles)
    chunk_cols = width // chunks
    chunk_tiles = tiles // chunks
    first = lax.axis_index("vocab") * width

    partial_latent = lax.dot_general(
        hidden, rank_factor, (((1,), (1,)), ((), ())), preferred_element_type=jnp.float32
    )
    latent = lax.psum(partial_latent, "vocab").astype(jnp.bfloat16)
    weight = cotangent.astype(jnp.float32) * lengths.astype(jnp.float32) / PREFIX_MAX
    target_local = targets - first
    row_words = jnp.repeat(grammar, row_count // grammar.shape[0], axis=0)

    peaks, sums, scores, hits = [], [], [], []
    for k in range(chunks):
        factor = lax.all_gather(
            vocab_factor[:, k * chunk_cols : (k + 1) * chunk_cols], "dp", axis=0, tiled=True
        )
        tile_ids = [k * chunk_tiles + t for t in range(chunk_tiles)]
        words = row_words[:, [t // WORD_BITS for t in tile_ids]]
        shifts = jnp.array([t % WORD_BITS for t in tile_ids], jnp.int32)
        bits = (jnp.right_shift(words, shifts[None, :]) & 1) == 1
        tile_on = jnp.broadcast_to(bits[:, :, None], (row_count, chunk_tiles, TILE)).reshape(
            row_count, chunk_cols
        )
        columns = k * chunk_cols + jnp.arange(chunk_cols, dtype=jnp.int32)
        target_hit = columns[None, :] == target_local[:, None]
        allowed = tile_on | target_hit
        logits = jnp.dot(latent, factor, preferred_element_type=jnp.float32)
        masked = jnp.where(allowed, logits, far_below)
        chunk_peak = jnp.max(masked, axis=1)
        powers = jnp.where(allowed, jnp.exp(masked - chunk_peak[:, None]), 0.0)
        peaks.append(chunk_peak)
        sums.append(jnp.sum(powers, axis=1))
        scores.append(
            lax.dot_general(
                powers.astype(jnp.bfloat16), factor, (((1,), (1,)), ((), ())),
                preferred_element_type=jnp.float32,
            )
        )
        hits.append(
            lax.dot_general(
                target_hit.astype(jnp.bfloat16), factor, (((1,), (1,)), ((), ())),
                preferred_element_type=jnp.float32,
            )
        )

    chunk_peaks = jnp.stack(peaks)
    peak = lax.pmax(jnp.max(chunk_peaks, axis=0), "vocab")
    scales = jnp.exp(chunk_peaks - peak[None, :])
    total = lax.psum(jnp.sum(jnp.stack(sums) * scales, axis=0), "vocab")
    expected = sum(scales[k][:, None] * scores[k] for k in range(chunks))
    target_rows = sum(hits)
    rank_partial = (weight / total)[:, None] * expected - weight[:, None] * target_rows
    rank_grad = lax.psum(rank_partial, "vocab").astype(jnp.bfloat16)

    grad_factor = lax.psum_scatter(
        lax.dot_general(
            rank_grad, hidden, (((0,), (0,)), ((), ())), preferred_element_type=jnp.float32
        ),
        "dp",
        scatter_dimension=0,
        tiled=True,
    )
    picked = jnp.take(rank_grad, assign, axis=0).reshape(groups, share, rank)
    slot_rank = lax.all_to_all(picked, "dp", split_axis=0, concat_axis=0, tiled=True).reshape(
        row_count, rank
    )
    grad_hidden = jnp.dot(slot_rank, rank_factor, preferred_element_type=jnp.float32).astype(
        jnp.bfloat16
    )
    return (grad_hidden, grad_factor)


def solution(mesh):
    return jax.shard_map(
        body,
        mesh=mesh,
        in_specs=(
            P("dp", "vocab"),
            P(None, "vocab"),
            P("dp", "vocab"),
            P("dp"),
            P("dp"),
            P("dp"),
            P("dp", "vocab"),
            P("dp"),
        ),
        out_specs=(P("dp", "vocab"), P("dp", "vocab")),
        check_vma=False,
    )
```

```python
import jax
import jax.numpy as jnp
from jax import lax
from jax.sharding import PartitionSpec as P

PREFIX_MAX = 4096


far_below = -1e30


def body(hidden, rank_factor, vocab_factor, lengths, targets, cotangent, grammar, assign):
    row_count = hidden.shape[0]
    rank = rank_factor.shape[0]
    groups = lax.axis_size("dp")
    share = row_count // groups
    width = vocab_factor.shape[1]
    tiles = width // 128
    first = lax.axis_index("vocab") * width
    factor = lax.all_gather(vocab_factor, "dp", axis=0, tiled=True)
    row_words = jnp.repeat(grammar, row_count // grammar.shape[0], axis=0)
    weight = cotangent.astype(jnp.float32) * lengths.astype(jnp.float32) / PREFIX_MAX

    partial_latent = lax.dot_general(
        hidden, rank_factor, (((1,), (1,)), ((), ())), preferred_element_type=jnp.float32
    )
    latent = lax.psum(partial_latent, "vocab").astype(jnp.bfloat16)
    target_local = targets - first
    columns = jnp.arange(width, dtype=jnp.int32)
    shifts = jnp.arange(30, dtype=jnp.int32)

    logits = jnp.dot(latent, factor, preferred_element_type=jnp.float32)
    bits = jnp.right_shift(row_words[:, :, None], shifts) & 1
    bits = bits.reshape(row_count, -1)[:, :tiles]
    tile_on = jnp.broadcast_to((bits == 1)[:, :, None], (row_count, tiles, 128)).reshape(
        row_count, width
    )
    target_hit = columns[None, :] == target_local[:, None]
    allowed = tile_on | target_hit
    masked = jnp.where(allowed, logits, far_below)
    peak = lax.pmax(jnp.max(masked, axis=1), "vocab")
    powers = jnp.where(allowed, jnp.exp(masked - peak[:, None]), 0.0)
    total = lax.psum(jnp.sum(powers, axis=1), "vocab")
    row_probs = powers / total[:, None]
    score_grad = (weight[:, None] * (row_probs - target_hit.astype(jnp.float32))).astype(
        jnp.bfloat16
    )
    rank_partial = lax.dot_general(
        score_grad, factor, (((1,), (1,)), ((), ())), preferred_element_type=jnp.float32
    )
    rank_grad = lax.psum(rank_partial, "vocab").astype(jnp.bfloat16)

    grad_factor = lax.psum_scatter(
        lax.dot_general(
            rank_grad, hidden, (((0,), (0,)), ((), ())), preferred_element_type=jnp.float32
        ),
        "dp",
        scatter_dimension=0,
        tiled=True,
    )
    picked = jnp.take(rank_grad, assign, axis=0).reshape(groups, share, rank)
    slot_rank = lax.all_to_all(picked, "dp", split_axis=0, concat_axis=0, tiled=True).reshape(
        row_count, rank
    )
    grad_hidden = jnp.dot(slot_rank, rank_factor, preferred_element_type=jnp.float32).astype(
        jnp.bfloat16
    )
    return (grad_hidden, grad_factor)


def solution(mesh):
    return jax.shard_map(
        body,
        mesh=mesh,
        in_specs=(
            P("dp", "vocab"),
            P(None, "vocab"),
            P("dp", "vocab"),
            P("dp"),
            P("dp"),
            P("dp"),
            P("dp", "vocab"),
            P("dp"),
        ),
        out_specs=(P("dp", "vocab"), P("dp", "vocab")),
        check_vma=False,
    )
```

```python
import jax
import jax.numpy as jnp
from jax import lax
from jax.sharding import PartitionSpec as P

PREFIX_MAX = 4096


far_below = -1e30


def body(hidden, rank_factor, vocab_factor, lengths, targets, cotangent, grammar, assign):
    row_count = hidden.shape[0]
    rank = rank_factor.shape[0]
    groups = lax.axis_size("dp")
    share = row_count // groups
    width = vocab_factor.shape[1]
    tiles = width // 128
    first = lax.axis_index("vocab") * width
    factor = lax.all_gather(vocab_factor, "dp", axis=0, tiled=True)
    row_words = jnp.repeat(grammar, row_count // grammar.shape[0], axis=0)
    weight = cotangent.astype(jnp.float32) * lengths.astype(jnp.float32) / PREFIX_MAX

    partial_latent = lax.dot_general(
        hidden, rank_factor, (((1,), (1,)), ((), ())), preferred_element_type=jnp.float32
    )
    latent = lax.psum(partial_latent, "vocab").astype(jnp.bfloat16)
    target_local = targets - first
    columns = jnp.arange(width, dtype=jnp.int32)
    shifts = jnp.arange(30, dtype=jnp.int32)

    logits = jnp.dot(latent, factor, preferred_element_type=jnp.float32)
    bits = jnp.right_shift(row_words[:, :, None], shifts) & 1
    bits = bits.reshape(row_count, -1)[:, :tiles]
    tile_on = jnp.broadcast_to((bits == 1)[:, :, None], (row_count, tiles, 128)).reshape(
        row_count, width
    )
    target_hit = columns[None, :] == target_local[:, None]
    allowed = tile_on | target_hit
    masked = jnp.where(allowed, logits, far_below)
    peak = lax.pmax(jnp.max(masked, axis=1), "vocab")
    powers = jnp.where(allowed, jnp.exp(masked - peak[:, None]), 0.0)
    total = lax.psum(jnp.sum(powers, axis=1), "vocab")
    row_probs = powers / total[:, None]
    score_grad = (weight[:, None] * (row_probs - target_hit.astype(jnp.float32))).astype(
        jnp.bfloat16
    )
    rank_partial = lax.dot_general(
        score_grad, factor, (((1,), (1,)), ((), ())), preferred_element_type=jnp.float32
    )
    rank_grad = lax.psum(rank_partial, "vocab").astype(jnp.bfloat16)

    grad_factor = lax.psum_scatter(
        lax.dot_general(
            rank_grad, hidden, (((0,), (0,)), ((), ())), preferred_element_type=jnp.float32
        ).astype(jnp.bfloat16),
        "dp",
        scatter_dimension=0,
        tiled=True,
    ).astype(jnp.float32)
    picked = jnp.take(rank_grad, assign, axis=0).reshape(groups, share, rank)
    slot_rank = lax.all_to_all(picked, "dp", split_axis=0, concat_axis=0, tiled=True).reshape(
        row_count, rank
    )
    grad_hidden = jnp.dot(slot_rank, rank_factor, preferred_element_type=jnp.float32).astype(
        jnp.bfloat16
    )
    return (grad_hidden, grad_factor)


def solution(mesh):
    return jax.shard_map(
        body,
        mesh=mesh,
        in_specs=(
            P("dp", "vocab"),
            P(None, "vocab"),
            P("dp", "vocab"),
            P("dp"),
            P("dp"),
            P("dp"),
            P("dp", "vocab"),
            P("dp"),
        ),
        out_specs=(P("dp", "vocab"), P("dp", "vocab")),
        check_vma=False,
    )
```

```python
import jax
import jax.numpy as jnp
from jax import lax
from jax.experimental import pallas as pl
from jax.experimental.pallas import tpu as pltpu
from jax.sharding import PartitionSpec as P
import functools

PREFIX_MAX = 4096


far_below = -1e30
TILE = 128


def block_mask(bits_ref, expand_ref, target_ref, block_cols):
    j = pl.program_id(0)
    tile_on = jnp.dot(bits_ref[...], expand_ref[...], preferred_element_type=jnp.float32) > 0.5
    columns = j * block_cols + lax.broadcasted_iota(jnp.int32, tile_on.shape, 1)
    target_hit = columns == target_ref[...]
    return tile_on | target_hit, target_hit


def stats_kernel(latent_ref, factor_ref, bits_ref, expand_ref, target_ref, peak_ref, total_ref, *, block_cols):
    @pl.when(pl.program_id(0) == 0)
    def _():
        peak_ref[...] = jnp.full(peak_ref.shape, far_below, jnp.float32)
        total_ref[...] = jnp.zeros(total_ref.shape, jnp.float32)

    allowed, _ = block_mask(bits_ref, expand_ref, target_ref, block_cols)
    logits = jnp.dot(latent_ref[...], factor_ref[...], preferred_element_type=jnp.float32)
    masked = jnp.where(allowed, logits, far_below)
    old = peak_ref[...]
    new = jnp.maximum(old, jnp.max(masked, axis=1, keepdims=True))
    powers = jnp.where(allowed, jnp.exp(masked - new), 0.0)
    total_ref[...] = total_ref[...] * jnp.exp(old - new) + jnp.sum(powers, axis=1, keepdims=True)
    peak_ref[...] = new


def grad_kernel(latent_ref, factor_ref, bits_ref, expand_ref, target_ref, peak_ref, total_ref, weight_ref,
                out_ref, *, block_cols):
    @pl.when(pl.program_id(0) == 0)
    def _():
        out_ref[...] = jnp.zeros(out_ref.shape, jnp.float32)

    allowed, target_hit = block_mask(bits_ref, expand_ref, target_ref, block_cols)
    logits = jnp.dot(latent_ref[...], factor_ref[...], preferred_element_type=jnp.float32)
    masked = jnp.where(allowed, logits, far_below)
    powers = jnp.where(allowed, jnp.exp(masked - peak_ref[...]), 0.0)
    row_probs = powers / total_ref[...]
    score_grad = (weight_ref[...] * (row_probs - target_hit.astype(jnp.float32))).astype(jnp.bfloat16)
    out_ref[...] += lax.dot_general(
        score_grad, factor_ref[...], (((1,), (1,)), ((), ())), preferred_element_type=jnp.float32
    )


def tiles_per_block(tiles):
    for count in (16, 8, 4, 2, 1):
        if tiles % count == 0:
            return count
    return 1


def softmax_parts(latent, factor, tile_bits, target_local):
    rows, rank = latent.shape
    width = factor.shape[1]
    tiles = width // TILE
    per_block = tiles_per_block(tiles)
    blocks = tiles // per_block
    block_cols = per_block * TILE
    padded = jnp.pad(tile_bits.reshape(rows, blocks, per_block), ((0, 0), (0, 0), (0, TILE - per_block)))
    bits = padded.reshape(rows, blocks * TILE).astype(jnp.bfloat16)
    expand = (
        lax.broadcasted_iota(jnp.int32, (TILE, block_cols), 0)
        == lax.broadcasted_iota(jnp.int32, (TILE, block_cols), 1) // TILE
    ).astype(jnp.bfloat16)
    target = target_local[:, None]
    common_specs = [
        pl.BlockSpec((rows, rank), lambda j: (0, 0)),
        pl.BlockSpec((rank, block_cols), lambda j: (0, j)),
        pl.BlockSpec((rows, TILE), lambda j: (0, j)),
        pl.BlockSpec((TILE, block_cols), lambda j: (0, 0)),
        pl.BlockSpec((rows, 1), lambda j: (0, 0)),
    ]
    column_spec = pl.BlockSpec((rows, 1), lambda j: (0, 0))
    params = pltpu.CompilerParams(dimension_semantics=("arbitrary",))
    matmul_flops = 2 * rows * rank * width + 2 * rows * TILE * width
    stats = pl.pallas_call(
        functools.partial(stats_kernel, block_cols=block_cols),
        grid=(blocks,),
        in_specs=common_specs,
        out_specs=[column_spec, column_spec],
        out_shape=[jax.ShapeDtypeStruct((rows, 1), jnp.float32)] * 2,
        compiler_params=params,
        cost_estimate=pl.CostEstimate(
            flops=matmul_flops, transcendentals=rows * width, bytes_accessed=rank * width * 2
        ),
    )

    def grads(peak, total, weight):
        return pl.pallas_call(
            functools.partial(grad_kernel, block_cols=block_cols),
            grid=(blocks,),
            in_specs=common_specs + [column_spec] * 3,
            out_specs=pl.BlockSpec((rows, rank), lambda j: (0, 0)),
            out_shape=jax.ShapeDtypeStruct((rows, rank), jnp.float32),
            compiler_params=params,
            cost_estimate=pl.CostEstimate(
                flops=matmul_flops + 2 * rows * rank * width,
                transcendentals=rows * width,
                bytes_accessed=rank * width * 2,
            ),
        )(latent, factor, bits, expand, target, peak, total, weight)

    peak, total = stats(latent, factor, bits, expand, target)
    return peak, total, grads


def body(hidden, rank_factor, vocab_factor, lengths, targets, cotangent, grammar, assign):
    row_count = hidden.shape[0]
    rank = rank_factor.shape[0]
    groups = lax.axis_size("dp")
    share = row_count // groups
    width = vocab_factor.shape[1]
    tiles = width // 128
    first = lax.axis_index("vocab") * width
    factor = lax.all_gather(vocab_factor, "dp", axis=0, tiled=True)
    row_words = jnp.repeat(grammar, row_count // grammar.shape[0], axis=0)
    weight = cotangent.astype(jnp.float32) * lengths.astype(jnp.float32) / PREFIX_MAX

    partial_latent = lax.dot_general(
        hidden, rank_factor, (((1,), (1,)), ((), ())), preferred_element_type=jnp.float32
    )
    latent = lax.psum(partial_latent, "vocab").astype(jnp.bfloat16)
    target_local = targets - first
    shifts = jnp.arange(30, dtype=jnp.int32)
    bits = jnp.right_shift(row_words[:, :, None], shifts) & 1
    tile_bits = bits.reshape(row_count, -1)[:, :tiles]
    local_peak, local_total, grads = softmax_parts(latent, factor, tile_bits, target_local)
    peak = lax.pmax(local_peak, "vocab")
    total = lax.psum(local_total * jnp.exp(local_peak - peak), "vocab")
    rank_partial = grads(peak, total, weight[:, None])
    rank_grad = lax.psum(rank_partial, "vocab").astype(jnp.bfloat16)

    grad_factor = lax.psum_scatter(
        lax.dot_general(
            rank_grad, hidden, (((0,), (0,)), ((), ())), preferred_element_type=jnp.float32
        ),
        "dp",
        scatter_dimension=0,
        tiled=True,
    )
    picked = jnp.take(rank_grad, assign, axis=0).reshape(groups, share, rank)
    slot_rank = lax.all_to_all(picked, "dp", split_axis=0, concat_axis=0, tiled=True).reshape(
        row_count, rank
    )
    grad_hidden = jnp.dot(slot_rank, rank_factor, preferred_element_type=jnp.float32).astype(
        jnp.bfloat16
    )
    return (grad_hidden, grad_factor)


def solution(mesh):
    return jax.shard_map(
        body,
        mesh=mesh,
        in_specs=(
            P("dp", "vocab"),
            P(None, "vocab"),
            P("dp", "vocab"),
            P("dp"),
            P("dp"),
            P("dp"),
            P("dp", "vocab"),
            P("dp"),
        ),
        out_specs=(P("dp", "vocab"), P("dp", "vocab")),
        check_vma=False,
    )
```

```python
import jax
import jax.numpy as jnp
from jax import lax
from jax.experimental import pallas as pl
from jax.experimental.pallas import tpu as pltpu
from jax.sharding import PartitionSpec as P
import functools

PREFIX_MAX = 4096


far_below = -1e30
TILE = 128


def block_scores(latent_ref, factor_ref, bias_ref, expand_ref, target_ref, block_cols):
    target_rel = target_ref[...] - pl.program_id(0) * block_cols
    bias = jnp.dot(bias_ref[...], expand_ref[...], preferred_element_type=jnp.float32)
    logits = jnp.dot(latent_ref[...], factor_ref[...], preferred_element_type=jnp.float32)
    target_hit = lax.broadcasted_iota(jnp.int32, logits.shape, 1) == target_rel
    return jnp.where(target_hit, logits, logits + bias), target_hit


def stats_kernel(latent_ref, factor_ref, bias_ref, expand_ref, target_ref, peak_ref, total_ref, *, block_cols):
    @pl.when(pl.program_id(0) == 0)
    def _():
        peak_ref[...] = jnp.full(peak_ref.shape, far_below, jnp.float32)
        total_ref[...] = jnp.zeros(total_ref.shape, jnp.float32)

    masked, _ = block_scores(latent_ref, factor_ref, bias_ref, expand_ref, target_ref, block_cols)
    old = peak_ref[...]
    new = jnp.maximum(old, jnp.max(masked, axis=1, keepdims=True))
    total_ref[...] = total_ref[...] * jnp.exp(old - new) + jnp.sum(
        jnp.exp(masked - new), axis=1, keepdims=True
    )
    peak_ref[...] = new


def grad_kernel(latent_ref, factor_ref, bias_ref, expand_ref, target_ref, peak_ref, scale_ref, weight_ref,
                out_ref, *, block_cols):
    @pl.when(pl.program_id(0) == 0)
    def _():
        out_ref[...] = jnp.zeros(out_ref.shape, jnp.float32)

    masked, target_hit = block_scores(latent_ref, factor_ref, bias_ref, expand_ref, target_ref, block_cols)
    powers = jnp.exp(masked - peak_ref[...])
    score_grad = (powers * scale_ref[...] - jnp.where(target_hit, weight_ref[...], 0.0)).astype(jnp.bfloat16)
    out_ref[...] += lax.dot_general(
        score_grad, factor_ref[...], (((1,), (1,)), ((), ())), preferred_element_type=jnp.float32
    )


def tiles_per_block(tiles):
    for count in (16, 8, 4, 2, 1):
        if tiles % count == 0:
            return count
    return 1


def softmax_parts(latent, factor, tile_bits, target_local):
    rows, rank = latent.shape
    width = factor.shape[1]
    tiles = width // TILE
    per_block = tiles_per_block(tiles)
    blocks = tiles // per_block
    block_cols = per_block * TILE
    padded = jnp.pad(tile_bits.reshape(rows, blocks, per_block), ((0, 0), (0, 0), (0, TILE - per_block)))
    bits = jnp.where(padded.reshape(rows, blocks * TILE) == 1, 0.0, far_below).astype(jnp.bfloat16)
    expand = (
        lax.broadcasted_iota(jnp.int32, (TILE, block_cols), 0)
        == lax.broadcasted_iota(jnp.int32, (TILE, block_cols), 1) // TILE
    ).astype(jnp.bfloat16)
    target = target_local[:, None]
    common_specs = [
        pl.BlockSpec((rows, rank), lambda j: (0, 0)),
        pl.BlockSpec((rank, block_cols), lambda j: (0, j)),
        pl.BlockSpec((rows, TILE), lambda j: (0, j)),
        pl.BlockSpec((TILE, block_cols), lambda j: (0, 0)),
        pl.BlockSpec((rows, 1), lambda j: (0, 0)),
    ]
    column_spec = pl.BlockSpec((rows, 1), lambda j: (0, 0))
    params = pltpu.CompilerParams(dimension_semantics=("arbitrary",))
    matmul_flops = 2 * rows * rank * width + 2 * rows * TILE * width
    stats = pl.pallas_call(
        functools.partial(stats_kernel, block_cols=block_cols),
        grid=(blocks,),
        in_specs=common_specs,
        out_specs=[column_spec, column_spec],
        out_shape=[jax.ShapeDtypeStruct((rows, 1), jnp.float32)] * 2,
        compiler_params=params,
        cost_estimate=pl.CostEstimate(
            flops=matmul_flops, transcendentals=rows * width, bytes_accessed=rank * width * 2
        ),
    )

    def grads(peak, scale, weight):
        return pl.pallas_call(
            functools.partial(grad_kernel, block_cols=block_cols),
            grid=(blocks,),
            in_specs=common_specs + [column_spec] * 3,
            out_specs=pl.BlockSpec((rows, rank), lambda j: (0, 0)),
            out_shape=jax.ShapeDtypeStruct((rows, rank), jnp.float32),
            compiler_params=params,
            cost_estimate=pl.CostEstimate(
                flops=matmul_flops + 2 * rows * rank * width,
                transcendentals=rows * width,
                bytes_accessed=rank * width * 2,
            ),
        )(latent, factor, bits, expand, target, peak, scale, weight)

    peak, total = stats(latent, factor, bits, expand, target)
    return peak, total, grads


def body(hidden, rank_factor, vocab_factor, lengths, targets, cotangent, grammar, assign):
    row_count = hidden.shape[0]
    rank = rank_factor.shape[0]
    groups = lax.axis_size("dp")
    share = row_count // groups
    width = vocab_factor.shape[1]
    tiles = width // 128
    first = lax.axis_index("vocab") * width
    factor = lax.all_gather(vocab_factor, "dp", axis=0, tiled=True)
    row_words = jnp.repeat(grammar, row_count // grammar.shape[0], axis=0)
    weight = cotangent.astype(jnp.float32) * lengths.astype(jnp.float32) / PREFIX_MAX

    partial_latent = lax.dot_general(
        hidden, rank_factor, (((1,), (1,)), ((), ())), preferred_element_type=jnp.float32
    )
    latent = lax.psum(partial_latent, "vocab").astype(jnp.bfloat16)
    target_local = targets - first
    shifts = jnp.arange(30, dtype=jnp.int32)
    bits = jnp.right_shift(row_words[:, :, None], shifts) & 1
    tile_bits = bits.reshape(row_count, -1)[:, :tiles]
    local_peak, local_total, grads = softmax_parts(latent, factor, tile_bits, target_local)
    local_peak = local_peak[:, 0]
    peak = lax.pmax(local_peak, "vocab")
    total = lax.psum(local_total[:, 0] * jnp.exp(local_peak - peak), "vocab")
    rank_partial = grads(peak[:, None], (weight / total)[:, None], weight[:, None])
    rank_grad = lax.psum(rank_partial, "vocab").astype(jnp.bfloat16)

    grad_factor = lax.psum_scatter(
        lax.dot_general(
            rank_grad, hidden, (((0,), (0,)), ((), ())), preferred_element_type=jnp.float32
        ),
        "dp",
        scatter_dimension=0,
        tiled=True,
    )
    picked = jnp.take(rank_grad, assign, axis=0).reshape(groups, share, rank)
    slot_rank = lax.all_to_all(picked, "dp", split_axis=0, concat_axis=0, tiled=True).reshape(
        row_count, rank
    )
    grad_hidden = jnp.dot(slot_rank, rank_factor, preferred_element_type=jnp.float32).astype(
        jnp.bfloat16
    )
    return (grad_hidden, grad_factor)


def solution(mesh):
    return jax.shard_map(
        body,
        mesh=mesh,
        in_specs=(
            P("dp", "vocab"),
            P(None, "vocab"),
            P("dp", "vocab"),
            P("dp"),
            P("dp"),
            P("dp"),
            P("dp", "vocab"),
            P("dp"),
        ),
        out_specs=(P("dp", "vocab"), P("dp", "vocab")),
        check_vma=False,
    )
```

```python
import jax
import jax.numpy as jnp
from jax import lax
from jax.experimental import pallas as pl
from jax.experimental.pallas import tpu as pltpu
from jax.sharding import PartitionSpec as P
import functools

PREFIX_MAX = 4096


far_below = -1e30
TILE = 128


def block_scores(latent_ref, factor_ref, bias_ref, expand_ref, target_ref, block_cols):
    target_rel = target_ref[...] - pl.program_id(0) * block_cols
    bias = jnp.dot(bias_ref[...], expand_ref[...], preferred_element_type=jnp.float32)
    logits = jnp.dot(latent_ref[...], factor_ref[...], preferred_element_type=jnp.float32)
    target_hit = lax.broadcasted_iota(jnp.int32, logits.shape, 1) == target_rel
    return jnp.where(target_hit, logits, logits + bias), target_hit


def stats_kernel(latent_ref, factor_ref, bias_ref, expand_ref, target_ref, peak_ref, total_ref, *, block_cols):
    @pl.when(pl.program_id(0) == 0)
    def _():
        peak_ref[...] = jnp.full(peak_ref.shape, far_below, jnp.float32)
        total_ref[...] = jnp.zeros(total_ref.shape, jnp.float32)

    masked, _ = block_scores(latent_ref, factor_ref, bias_ref, expand_ref, target_ref, block_cols)
    old = peak_ref[...]
    new = jnp.maximum(old, jnp.max(masked, axis=1, keepdims=True))
    total_ref[...] = total_ref[...] * jnp.exp(old - new) + jnp.sum(
        jnp.exp(masked - new), axis=1, keepdims=True
    )
    peak_ref[...] = new


def grad_kernel(latent_ref, factor_ref, bias_ref, expand_ref, target_ref, peak_ref, scale_ref, weight_ref,
                out_ref, *, block_cols):
    @pl.when(pl.program_id(0) == 0)
    def _():
        out_ref[...] = jnp.zeros(out_ref.shape, jnp.float32)

    masked, target_hit = block_scores(latent_ref, factor_ref, bias_ref, expand_ref, target_ref, block_cols)
    powers = jnp.exp(masked - peak_ref[...])
    score_grad = (powers * scale_ref[...] - jnp.where(target_hit, weight_ref[...], 0.0)).astype(jnp.bfloat16)
    out_ref[...] += lax.dot_general(
        score_grad, factor_ref[...], (((1,), (1,)), ((), ())), preferred_element_type=jnp.float32
    )


def tiles_per_block(tiles):
    for count in (38, 19, 16, 8, 4, 2, 1):
        if tiles % count == 0:
            return count
    return 1


def softmax_parts(latent, factor, tile_bits, target_local):
    rows, rank = latent.shape
    width = factor.shape[1]
    tiles = width // TILE
    per_block = tiles_per_block(tiles)
    blocks = tiles // per_block
    block_cols = per_block * TILE
    padded = jnp.pad(tile_bits.reshape(rows, blocks, per_block), ((0, 0), (0, 0), (0, TILE - per_block)))
    bits = jnp.where(padded.reshape(rows, blocks * TILE) == 1, 0.0, far_below).astype(jnp.bfloat16)
    expand = (
        lax.broadcasted_iota(jnp.int32, (TILE, block_cols), 0)
        == lax.broadcasted_iota(jnp.int32, (TILE, block_cols), 1) // TILE
    ).astype(jnp.bfloat16)
    target = target_local[:, None]
    common_specs = [
        pl.BlockSpec((rows, rank), lambda j: (0, 0)),
        pl.BlockSpec((rank, block_cols), lambda j: (0, j)),
        pl.BlockSpec((rows, TILE), lambda j: (0, j)),
        pl.BlockSpec((TILE, block_cols), lambda j: (0, 0)),
        pl.BlockSpec((rows, 1), lambda j: (0, 0)),
    ]
    column_spec = pl.BlockSpec((rows, 1), lambda j: (0, 0))
    params = pltpu.CompilerParams(dimension_semantics=("arbitrary",))
    matmul_flops = 2 * rows * rank * width + 2 * rows * TILE * width
    stats = pl.pallas_call(
        functools.partial(stats_kernel, block_cols=block_cols),
        grid=(blocks,),
        in_specs=common_specs,
        out_specs=[column_spec, column_spec],
        out_shape=[jax.ShapeDtypeStruct((rows, 1), jnp.float32)] * 2,
        compiler_params=params,
        cost_estimate=pl.CostEstimate(
            flops=matmul_flops, transcendentals=rows * width, bytes_accessed=rank * width * 2
        ),
    )

    def grads(peak, scale, weight):
        return pl.pallas_call(
            functools.partial(grad_kernel, block_cols=block_cols),
            grid=(blocks,),
            in_specs=common_specs + [column_spec] * 3,
            out_specs=pl.BlockSpec((rows, rank), lambda j: (0, 0)),
            out_shape=jax.ShapeDtypeStruct((rows, rank), jnp.float32),
            compiler_params=params,
            cost_estimate=pl.CostEstimate(
                flops=matmul_flops + 2 * rows * rank * width,
                transcendentals=rows * width,
                bytes_accessed=rank * width * 2,
            ),
        )(latent, factor, bits, expand, target, peak, scale, weight)

    peak, total = stats(latent, factor, bits, expand, target)
    return peak, total, grads


def body(hidden, rank_factor, vocab_factor, lengths, targets, cotangent, grammar, assign):
    row_count = hidden.shape[0]
    rank = rank_factor.shape[0]
    groups = lax.axis_size("dp")
    share = row_count // groups
    width = vocab_factor.shape[1]
    tiles = width // 128
    first = lax.axis_index("vocab") * width
    factor = lax.all_gather(vocab_factor, "dp", axis=0, tiled=True)
    row_words = jnp.repeat(grammar, row_count // grammar.shape[0], axis=0)
    weight = cotangent.astype(jnp.float32) * lengths.astype(jnp.float32) / PREFIX_MAX

    partial_latent = lax.dot_general(
        hidden, rank_factor, (((1,), (1,)), ((), ())), preferred_element_type=jnp.float32
    )
    latent = lax.psum(partial_latent, "vocab").astype(jnp.bfloat16)
    target_local = targets - first
    shifts = jnp.arange(30, dtype=jnp.int32)
    bits = jnp.right_shift(row_words[:, :, None], shifts) & 1
    tile_bits = bits.reshape(row_count, -1)[:, :tiles]
    local_peak, local_total, grads = softmax_parts(latent, factor, tile_bits, target_local)
    local_peak = local_peak[:, 0]
    peak = lax.pmax(local_peak, "vocab")
    total = lax.psum(local_total[:, 0] * jnp.exp(local_peak - peak), "vocab")
    rank_partial = grads(peak[:, None], (weight / total)[:, None], weight[:, None])
    rank_grad = lax.psum(rank_partial, "vocab").astype(jnp.bfloat16)

    grad_factor = lax.psum_scatter(
        lax.dot_general(
            rank_grad, hidden, (((0,), (0,)), ((), ())), preferred_element_type=jnp.float32
        ),
        "dp",
        scatter_dimension=0,
        tiled=True,
    )
    picked = jnp.take(rank_grad, assign, axis=0).reshape(groups, share, rank)
    slot_rank = lax.all_to_all(picked, "dp", split_axis=0, concat_axis=0, tiled=True).reshape(
        row_count, rank
    )
    grad_hidden = jnp.dot(slot_rank, rank_factor, preferred_element_type=jnp.float32).astype(
        jnp.bfloat16
    )
    return (grad_hidden, grad_factor)


def solution(mesh):
    return jax.shard_map(
        body,
        mesh=mesh,
        in_specs=(
            P("dp", "vocab"),
            P(None, "vocab"),
            P("dp", "vocab"),
            P("dp"),
            P("dp"),
            P("dp"),
            P("dp", "vocab"),
            P("dp"),
        ),
        out_specs=(P("dp", "vocab"), P("dp", "vocab")),
        check_vma=False,
    )
```

```python
import jax
import jax.numpy as jnp
from jax import lax
from jax.experimental import pallas as pl
from jax.experimental.pallas import tpu as pltpu
from jax.sharding import PartitionSpec as P
import functools

PREFIX_MAX = 4096


far_below = -1e30
TILE = 128


def block_scores(latent_ref, factor_ref, bias_ref, expand_ref, target_ref, block_cols):
    target_rel = target_ref[...] - pl.program_id(0) * block_cols
    bias = jnp.dot(bias_ref[...], expand_ref[...], preferred_element_type=jnp.float32)
    logits = jnp.dot(latent_ref[...], factor_ref[...], preferred_element_type=jnp.float32)
    target_hit = lax.broadcasted_iota(jnp.int32, logits.shape, 1) == target_rel
    return jnp.where(target_hit, logits, logits + bias), target_hit


def stats_kernel(latent_ref, factor_ref, bias_ref, expand_ref, target_ref, peak_ref, total_ref, *, block_cols):
    @pl.when(pl.program_id(0) == 0)
    def _():
        peak_ref[...] = jnp.full(peak_ref.shape, far_below, jnp.float32)
        total_ref[...] = jnp.zeros(total_ref.shape, jnp.float32)

    masked, _ = block_scores(latent_ref, factor_ref, bias_ref, expand_ref, target_ref, block_cols)
    old = peak_ref[...]
    new = jnp.maximum(old, jnp.max(masked, axis=1, keepdims=True))
    total_ref[...] = total_ref[...] * jnp.exp(old - new) + jnp.sum(
        jnp.exp(masked - new), axis=1, keepdims=True
    )
    peak_ref[...] = new


def grad_kernel(latent_ref, factor_ref, bias_ref, expand_ref, target_ref, peak_ref, scale_ref, weight_ref,
                out_ref, *, block_cols):
    @pl.when(pl.program_id(0) == 0)
    def _():
        out_ref[...] = jnp.zeros(out_ref.shape, jnp.float32)

    masked, target_hit = block_scores(latent_ref, factor_ref, bias_ref, expand_ref, target_ref, block_cols)
    powers = jnp.exp(masked - peak_ref[...])
    score_grad = (powers * scale_ref[...] - jnp.where(target_hit, weight_ref[...], 0.0)).astype(jnp.bfloat16)
    out_ref[...] += lax.dot_general(
        score_grad, factor_ref[...], (((1,), (1,)), ((), ())), preferred_element_type=jnp.float32
    )


def tiles_per_block(tiles):
    for count in (76, 38, 19, 16, 8, 4, 2, 1):
        if tiles % count == 0:
            return count
    return 1


def softmax_parts(latent, factor, tile_bits, target_local):
    rows, rank = latent.shape
    width = factor.shape[1]
    tiles = width // TILE
    per_block = tiles_per_block(tiles)
    blocks = tiles // per_block
    block_cols = per_block * TILE
    padded = jnp.pad(tile_bits.reshape(rows, blocks, per_block), ((0, 0), (0, 0), (0, TILE - per_block)))
    bits = jnp.where(padded.reshape(rows, blocks * TILE) == 1, 0.0, far_below).astype(jnp.bfloat16)
    expand = (
        lax.broadcasted_iota(jnp.int32, (TILE, block_cols), 0)
        == lax.broadcasted_iota(jnp.int32, (TILE, block_cols), 1) // TILE
    ).astype(jnp.bfloat16)
    target = target_local[:, None]
    common_specs = [
        pl.BlockSpec((rows, rank), lambda j: (0, 0)),
        pl.BlockSpec((rank, block_cols), lambda j: (0, j)),
        pl.BlockSpec((rows, TILE), lambda j: (0, j)),
        pl.BlockSpec((TILE, block_cols), lambda j: (0, 0)),
        pl.BlockSpec((rows, 1), lambda j: (0, 0)),
    ]
    column_spec = pl.BlockSpec((rows, 1), lambda j: (0, 0))
    params = pltpu.CompilerParams(dimension_semantics=("arbitrary",))
    matmul_flops = 2 * rows * rank * width + 2 * rows * TILE * width
    stats = pl.pallas_call(
        functools.partial(stats_kernel, block_cols=block_cols),
        grid=(blocks,),
        in_specs=common_specs,
        out_specs=[column_spec, column_spec],
        out_shape=[jax.ShapeDtypeStruct((rows, 1), jnp.float32)] * 2,
        compiler_params=params,
        cost_estimate=pl.CostEstimate(
            flops=matmul_flops, transcendentals=rows * width, bytes_accessed=rank * width * 2
        ),
    )

    def grads(peak, scale, weight):
        return pl.pallas_call(
            functools.partial(grad_kernel, block_cols=block_cols),
            grid=(blocks,),
            in_specs=common_specs + [column_spec] * 3,
            out_specs=pl.BlockSpec((rows, rank), lambda j: (0, 0)),
            out_shape=jax.ShapeDtypeStruct((rows, rank), jnp.float32),
            compiler_params=params,
            cost_estimate=pl.CostEstimate(
                flops=matmul_flops + 2 * rows * rank * width,
                transcendentals=rows * width,
                bytes_accessed=rank * width * 2,
            ),
        )(latent, factor, bits, expand, target, peak, scale, weight)

    peak, total = stats(latent, factor, bits, expand, target)
    return peak, total, grads


def body(hidden, rank_factor, vocab_factor, lengths, targets, cotangent, grammar, assign):
    row_count = hidden.shape[0]
    rank = rank_factor.shape[0]
    groups = lax.axis_size("dp")
    share = row_count // groups
    width = vocab_factor.shape[1]
    tiles = width // 128
    first = lax.axis_index("vocab") * width
    factor = lax.all_gather(vocab_factor, "dp", axis=0, tiled=True)
    row_words = jnp.repeat(grammar, row_count // grammar.shape[0], axis=0)
    weight = cotangent.astype(jnp.float32) * lengths.astype(jnp.float32) / PREFIX_MAX

    partial_latent = lax.dot_general(
        hidden, rank_factor, (((1,), (1,)), ((), ())), preferred_element_type=jnp.float32
    )
    latent = lax.psum(partial_latent, "vocab").astype(jnp.bfloat16)
    target_local = targets - first
    shifts = jnp.arange(30, dtype=jnp.int32)
    bits = jnp.right_shift(row_words[:, :, None], shifts) & 1
    tile_bits = bits.reshape(row_count, -1)[:, :tiles]
    local_peak, local_total, grads = softmax_parts(latent, factor, tile_bits, target_local)
    local_peak = local_peak[:, 0]
    peak = lax.pmax(local_peak, "vocab")
    total = lax.psum(local_total[:, 0] * jnp.exp(local_peak - peak), "vocab")
    rank_partial = grads(peak[:, None], (weight / total)[:, None], weight[:, None])
    rank_grad = lax.psum(rank_partial, "vocab").astype(jnp.bfloat16)

    grad_factor = lax.psum_scatter(
        lax.dot_general(
            rank_grad, hidden, (((0,), (0,)), ((), ())), preferred_element_type=jnp.float32
        ),
        "dp",
        scatter_dimension=0,
        tiled=True,
    )
    picked = jnp.take(rank_grad, assign, axis=0).reshape(groups, share, rank)
    slot_rank = lax.all_to_all(picked, "dp", split_axis=0, concat_axis=0, tiled=True).reshape(
        row_count, rank
    )
    grad_hidden = jnp.dot(slot_rank, rank_factor, preferred_element_type=jnp.float32).astype(
        jnp.bfloat16
    )
    return (grad_hidden, grad_factor)


def solution(mesh):
    return jax.shard_map(
        body,
        mesh=mesh,
        in_specs=(
            P("dp", "vocab"),
            P(None, "vocab"),
            P("dp", "vocab"),
            P("dp"),
            P("dp"),
            P("dp"),
            P("dp", "vocab"),
            P("dp"),
        ),
        out_specs=(P("dp", "vocab"), P("dp", "vocab")),
        check_vma=False,
    )
```

```python
import jax
import jax.numpy as jnp
from jax import lax
from jax.experimental import pallas as pl
from jax.experimental.pallas import tpu as pltpu
from jax.sharding import PartitionSpec as P
import functools

PREFIX_MAX = 4096


far_below = -1e30
TILE = 128


def block_scores(latent_ref, factor_ref, bias_ref, expand_ref, target_ref, block_cols):
    target_rel = target_ref[...] - pl.program_id(0) * block_cols
    bias = jnp.dot(bias_ref[...], expand_ref[...], preferred_element_type=jnp.float32)
    logits = jnp.dot(latent_ref[...], factor_ref[...], preferred_element_type=jnp.float32)
    target_hit = lax.broadcasted_iota(jnp.int32, logits.shape, 1) == target_rel
    return jnp.where(target_hit, logits, logits + bias), target_hit


def stats_kernel(latent_ref, factor_ref, bias_ref, expand_ref, target_ref, peak_ref, total_ref, *, block_cols):
    @pl.when(pl.program_id(0) == 0)
    def _():
        peak_ref[...] = jnp.full(peak_ref.shape, far_below, jnp.float32)
        total_ref[...] = jnp.zeros(total_ref.shape, jnp.float32)

    masked, _ = block_scores(latent_ref, factor_ref, bias_ref, expand_ref, target_ref, block_cols)
    old = peak_ref[...]
    new = jnp.maximum(old, jnp.max(masked, axis=1, keepdims=True))
    total_ref[...] = total_ref[...] * jnp.exp(old - new) + jnp.sum(
        jnp.exp(masked - new), axis=1, keepdims=True
    )
    peak_ref[...] = new


def grad_kernel(latent_ref, factor_ref, bias_ref, expand_ref, target_ref, peak_ref, scale_ref, weight_ref,
                out_ref, *, block_cols):
    @pl.when(pl.program_id(0) == 0)
    def _():
        out_ref[...] = jnp.zeros(out_ref.shape, jnp.float32)

    masked, target_hit = block_scores(latent_ref, factor_ref, bias_ref, expand_ref, target_ref, block_cols)
    powers = jnp.exp(masked - peak_ref[...])
    score_grad = (powers * scale_ref[...] - jnp.where(target_hit, weight_ref[...], 0.0)).astype(jnp.bfloat16)
    out_ref[...] += lax.dot_general(
        score_grad, factor_ref[...], (((1,), (1,)), ((), ())), preferred_element_type=jnp.float32
    )


def tiles_per_block(tiles):
    for count in (38, 19, 16, 8, 4, 2, 1):
        if tiles % count == 0:
            return count
    return 1


def softmax_parts(latent, factor, tile_bits, target_local):
    rows, rank = latent.shape
    width = factor.shape[1]
    tiles = width // TILE
    per_block = tiles_per_block(tiles)
    blocks = tiles // per_block
    block_cols = per_block * TILE
    padded = jnp.pad(tile_bits.reshape(rows, blocks, per_block), ((0, 0), (0, 0), (0, TILE - per_block)))
    bits = jnp.where(padded.reshape(rows, blocks * TILE) == 1, 0.0, far_below).astype(jnp.bfloat16)
    expand = (
        lax.broadcasted_iota(jnp.int32, (TILE, block_cols), 0)
        == lax.broadcasted_iota(jnp.int32, (TILE, block_cols), 1) // TILE
    ).astype(jnp.bfloat16)
    target = target_local[:, None]
    common_specs = [
        pl.BlockSpec((rows, rank), lambda j: (0, 0)),
        pl.BlockSpec((rank, block_cols), lambda j: (0, j)),
        pl.BlockSpec((rows, TILE), lambda j: (0, j)),
        pl.BlockSpec((TILE, block_cols), lambda j: (0, 0)),
        pl.BlockSpec((rows, 1), lambda j: (0, 0)),
    ]
    column_spec = pl.BlockSpec((rows, 1), lambda j: (0, 0))
    params = pltpu.CompilerParams(dimension_semantics=("arbitrary",))
    matmul_flops = 2 * rows * rank * width + 2 * rows * TILE * width
    stats = pl.pallas_call(
        functools.partial(stats_kernel, block_cols=block_cols),
        grid=(blocks,),
        in_specs=common_specs,
        out_specs=[column_spec, column_spec],
        out_shape=[jax.ShapeDtypeStruct((rows, 1), jnp.float32)] * 2,
        compiler_params=params,
        cost_estimate=pl.CostEstimate(
            flops=matmul_flops, transcendentals=rows * width, bytes_accessed=rank * width * 2
        ),
    )

    def grads(peak, scale, weight):
        return pl.pallas_call(
            functools.partial(grad_kernel, block_cols=block_cols),
            grid=(blocks,),
            in_specs=common_specs + [column_spec] * 3,
            out_specs=pl.BlockSpec((rows, rank), lambda j: (0, 0)),
            out_shape=jax.ShapeDtypeStruct((rows, rank), jnp.float32),
            compiler_params=params,
            cost_estimate=pl.CostEstimate(
                flops=matmul_flops + 2 * rows * rank * width,
                transcendentals=rows * width,
                bytes_accessed=rank * width * 2,
            ),
        )(latent, factor, bits, expand, target, peak, scale, weight)

    peak, total = stats(latent, factor, bits, expand, target)
    return peak, total, grads


def body(hidden, rank_factor, vocab_factor, lengths, targets, cotangent, grammar, assign):
    row_count = hidden.shape[0]
    rank = rank_factor.shape[0]
    groups = lax.axis_size("dp")
    share = row_count // groups
    width = vocab_factor.shape[1]
    tiles = width // 128
    first = lax.axis_index("vocab") * width
    pair = lax.axis_size("vocab") == 2

    def partner(x):
        return lax.ppermute(x, "vocab", perm=[(0, 1), (1, 0)])

    factor = lax.all_gather(vocab_factor, "dp", axis=0, tiled=True)
    row_words = jnp.repeat(grammar, row_count // grammar.shape[0], axis=0)
    weight = cotangent.astype(jnp.float32) * lengths.astype(jnp.float32) / PREFIX_MAX

    partial_latent = lax.dot_general(
        hidden, rank_factor, (((1,), (1,)), ((), ())), preferred_element_type=jnp.float32
    )
    latent = lax.psum(partial_latent, "vocab").astype(jnp.bfloat16)
    target_local = targets - first
    shifts = jnp.arange(30, dtype=jnp.int32)
    bits = jnp.right_shift(row_words[:, :, None], shifts) & 1
    tile_bits = bits.reshape(row_count, -1)[:, :tiles]
    local_peak, local_total, grads = softmax_parts(latent, factor, tile_bits, target_local)
    local_peak = local_peak[:, 0]
    local_total = local_total[:, 0]
    if pair:
        other_peak, other_total = partner(jnp.stack([local_peak, local_total]))
        peak = jnp.maximum(local_peak, other_peak)
        total = local_total * jnp.exp(local_peak - peak) + other_total * jnp.exp(other_peak - peak)
    else:
        peak = lax.pmax(local_peak, "vocab")
        total = lax.psum(local_total * jnp.exp(local_peak - peak), "vocab")
    rank_partial = grads(peak[:, None], (weight / total)[:, None], weight[:, None])
    if pair:
        rank_grad = (rank_partial + partner(rank_partial)).astype(jnp.bfloat16)
    else:
        rank_grad = lax.psum(rank_partial, "vocab").astype(jnp.bfloat16)

    grad_factor = lax.psum_scatter(
        lax.dot_general(
            rank_grad, hidden, (((0,), (0,)), ((), ())), preferred_element_type=jnp.float32
        ),
        "dp",
        scatter_dimension=0,
        tiled=True,
    )
    picked = jnp.take(rank_grad, assign, axis=0).reshape(groups, share, rank)
    slot_rank = lax.all_to_all(picked, "dp", split_axis=0, concat_axis=0, tiled=True).reshape(
        row_count, rank
    )
    grad_hidden = jnp.dot(slot_rank, rank_factor, preferred_element_type=jnp.float32).astype(
        jnp.bfloat16
    )
    return (grad_hidden, grad_factor)


def solution(mesh):
    return jax.shard_map(
        body,
        mesh=mesh,
        in_specs=(
            P("dp", "vocab"),
            P(None, "vocab"),
            P("dp", "vocab"),
            P("dp"),
            P("dp"),
            P("dp"),
            P("dp", "vocab"),
            P("dp"),
        ),
        out_specs=(P("dp", "vocab"), P("dp", "vocab")),
        check_vma=False,
    )
```

```python
import jax
import jax.numpy as jnp
from jax import lax
from jax.experimental import pallas as pl
from jax.experimental.pallas import tpu as pltpu
from jax.sharding import PartitionSpec as P
import functools

PREFIX_MAX = 4096


far_below = -1e30
TILE = 128


def block_scores(latent_ref, factor_ref, bias_ref, expand_ref, target_ref, block_cols):
    target_rel = target_ref[...] - pl.program_id(0) * block_cols
    bias = jnp.dot(bias_ref[...], expand_ref[...], preferred_element_type=jnp.float32)
    logits = jnp.dot(latent_ref[...], factor_ref[...], preferred_element_type=jnp.float32)
    target_hit = lax.broadcasted_iota(jnp.int32, logits.shape, 1) == target_rel
    return jnp.where(target_hit, logits, logits + bias), target_hit


def stats_kernel(latent_ref, factor_ref, bias_ref, expand_ref, target_ref, peak_ref, total_ref, *, block_cols):
    @pl.when(pl.program_id(0) == 0)
    def _():
        peak_ref[...] = jnp.full(peak_ref.shape, far_below, jnp.float32)
        total_ref[...] = jnp.zeros(total_ref.shape, jnp.float32)

    masked, _ = block_scores(latent_ref, factor_ref, bias_ref, expand_ref, target_ref, block_cols)
    old = peak_ref[...]
    new = jnp.maximum(old, jnp.max(masked, axis=1, keepdims=True))
    total_ref[...] = total_ref[...] * jnp.exp(old - new) + jnp.sum(
        jnp.exp(masked - new), axis=1, keepdims=True
    )
    peak_ref[...] = new


def grad_kernel(latent_ref, factor_ref, bias_ref, expand_ref, target_ref, peak_ref, scale_ref, weight_ref,
                out_ref, *, block_cols):
    @pl.when(pl.program_id(0) == 0)
    def _():
        out_ref[...] = jnp.zeros(out_ref.shape, jnp.float32)

    masked, target_hit = block_scores(latent_ref, factor_ref, bias_ref, expand_ref, target_ref, block_cols)
    powers = jnp.exp(masked - peak_ref[...])
    score_grad = (powers * scale_ref[...] - jnp.where(target_hit, weight_ref[...], 0.0)).astype(jnp.bfloat16)
    out_ref[...] += lax.dot_general(
        score_grad, factor_ref[...], (((1,), (1,)), ((), ())), preferred_element_type=jnp.float32
    )


def tiles_per_block(tiles):
    for count in (38, 19, 16, 8, 4, 2, 1):
        if tiles % count == 0:
            return count
    return 1


def softmax_parts(latent, factor, tile_bits, target_local):
    rows, rank = latent.shape
    width = factor.shape[1]
    tiles = width // TILE
    per_block = tiles_per_block(tiles)
    blocks = tiles // per_block
    block_cols = per_block * TILE
    padded = jnp.pad(tile_bits.reshape(rows, blocks, per_block), ((0, 0), (0, 0), (0, TILE - per_block)))
    bits = jnp.where(padded.reshape(rows, blocks * TILE) == 1, 0.0, far_below).astype(jnp.bfloat16)
    expand = (
        lax.broadcasted_iota(jnp.int32, (TILE, block_cols), 0)
        == lax.broadcasted_iota(jnp.int32, (TILE, block_cols), 1) // TILE
    ).astype(jnp.bfloat16)
    target = target_local[:, None]
    common_specs = [
        pl.BlockSpec((rows, rank), lambda j: (0, 0)),
        pl.BlockSpec((rank, block_cols), lambda j: (0, j)),
        pl.BlockSpec((rows, TILE), lambda j: (0, j)),
        pl.BlockSpec((TILE, block_cols), lambda j: (0, 0)),
        pl.BlockSpec((rows, 1), lambda j: (0, 0)),
    ]
    column_spec = pl.BlockSpec((rows, 1), lambda j: (0, 0))
    params = pltpu.CompilerParams(dimension_semantics=("arbitrary",))
    matmul_flops = 2 * rows * rank * width + 2 * rows * TILE * width
    stats = pl.pallas_call(
        functools.partial(stats_kernel, block_cols=block_cols),
        grid=(blocks,),
        in_specs=common_specs,
        out_specs=[column_spec, column_spec],
        out_shape=[jax.ShapeDtypeStruct((rows, 1), jnp.float32)] * 2,
        compiler_params=params,
        cost_estimate=pl.CostEstimate(
            flops=matmul_flops, transcendentals=rows * width, bytes_accessed=rank * width * 2
        ),
    )

    def grads(peak, scale, weight):
        return pl.pallas_call(
            functools.partial(grad_kernel, block_cols=block_cols),
            grid=(blocks,),
            in_specs=common_specs + [column_spec] * 3,
            out_specs=pl.BlockSpec((rows, rank), lambda j: (0, 0)),
            out_shape=jax.ShapeDtypeStruct((rows, rank), jnp.float32),
            compiler_params=params,
            cost_estimate=pl.CostEstimate(
                flops=matmul_flops + 2 * rows * rank * width,
                transcendentals=rows * width,
                bytes_accessed=rank * width * 2,
            ),
        )(latent, factor, bits, expand, target, peak, scale, weight)

    peak, total = stats(latent, factor, bits, expand, target)
    return peak, total, grads


def body(hidden, rank_factor, vocab_factor, lengths, targets, cotangent, grammar, assign):
    row_count = hidden.shape[0]
    rank = rank_factor.shape[0]
    groups = lax.axis_size("dp")
    share = row_count // groups
    width = vocab_factor.shape[1]
    tiles = width // 128
    first = lax.axis_index("vocab") * width
    pair = lax.axis_size("vocab") == 2

    def partner(x):
        return lax.ppermute(x, "vocab", perm=[(0, 1), (1, 0)])

    factor = lax.all_gather(vocab_factor, "dp", axis=0, tiled=True)
    row_words = jnp.repeat(grammar, row_count // grammar.shape[0], axis=0)
    weight = (cotangent.astype(jnp.float32) * lengths.astype(jnp.float32) / PREFIX_MAX)[:, None]

    partial_latent = lax.dot_general(
        hidden, rank_factor, (((1,), (1,)), ((), ())), preferred_element_type=jnp.float32
    )
    latent = lax.psum(partial_latent, "vocab").astype(jnp.bfloat16)
    target_local = targets - first
    shifts = jnp.arange(30, dtype=jnp.int32)
    bits = jnp.right_shift(row_words[:, :, None], shifts) & 1
    tile_bits = bits.reshape(row_count, -1)[:, :tiles]
    local_peak, local_total, grads = softmax_parts(latent, factor, tile_bits, target_local)
    if pair:
        other_peak, other_total = partner(local_peak), partner(local_total)
        peak = jnp.maximum(local_peak, other_peak)
        total = local_total * jnp.exp(local_peak - peak) + other_total * jnp.exp(other_peak - peak)
    else:
        peak = lax.pmax(local_peak, "vocab")
        total = lax.psum(local_total * jnp.exp(local_peak - peak), "vocab")
    rank_partial = grads(peak, weight / total, weight)
    if pair:
        rank_grad = (rank_partial + partner(rank_partial)).astype(jnp.bfloat16)
    else:
        rank_grad = lax.psum(rank_partial, "vocab").astype(jnp.bfloat16)

    grad_factor = lax.psum_scatter(
        lax.dot_general(
            rank_grad, hidden, (((0,), (0,)), ((), ())), preferred_element_type=jnp.float32
        ),
        "dp",
        scatter_dimension=0,
        tiled=True,
    )
    picked = jnp.take(rank_grad, assign, axis=0).reshape(groups, share, rank)
    slot_rank = lax.all_to_all(picked, "dp", split_axis=0, concat_axis=0, tiled=True).reshape(
        row_count, rank
    )
    grad_hidden = jnp.dot(slot_rank, rank_factor, preferred_element_type=jnp.float32).astype(
        jnp.bfloat16
    )
    return (grad_hidden, grad_factor)


def solution(mesh):
    return jax.shard_map(
        body,
        mesh=mesh,
        in_specs=(
            P("dp", "vocab"),
            P(None, "vocab"),
            P("dp", "vocab"),
            P("dp"),
            P("dp"),
            P("dp"),
            P("dp", "vocab"),
            P("dp"),
        ),
        out_specs=(P("dp", "vocab"), P("dp", "vocab")),
        check_vma=False,
    )
```

```python
import jax
import jax.numpy as jnp
from jax import lax
from jax.experimental import pallas as pl
from jax.experimental.pallas import tpu as pltpu
from jax.sharding import PartitionSpec as P
import functools

PREFIX_MAX = 4096


far_below = -1e30
TILE = 128


def block_scores(latent_ref, factor_ref, bias_ref, expand_ref, target_ref, block_cols):
    target_rel = target_ref[...] - pl.program_id(0) * block_cols
    bias = jnp.dot(bias_ref[...], expand_ref[...], preferred_element_type=jnp.float32)
    logits = jnp.dot(latent_ref[...], factor_ref[...], preferred_element_type=jnp.float32)
    target_hit = lax.broadcasted_iota(jnp.int32, logits.shape, 1) == target_rel
    return jnp.where(target_hit, logits, logits + bias), target_hit


def stats_kernel(latent_ref, factor_ref, bias_ref, expand_ref, target_ref, peak_ref, total_ref, *, block_cols):
    @pl.when(pl.program_id(0) == 0)
    def _():
        peak_ref[...] = jnp.full(peak_ref.shape, far_below, jnp.float32)
        total_ref[...] = jnp.zeros(total_ref.shape, jnp.float32)

    masked, _ = block_scores(latent_ref, factor_ref, bias_ref, expand_ref, target_ref, block_cols)
    old = peak_ref[...]
    new = jnp.maximum(old, jnp.max(masked, axis=1, keepdims=True))
    total_ref[...] = total_ref[...] * jnp.exp(old - new) + jnp.sum(
        jnp.exp(masked - new), axis=1, keepdims=True
    )
    peak_ref[...] = new


def grad_kernel(latent_ref, factor_ref, bias_ref, expand_ref, target_ref, peak_ref, scale_ref, weight_ref,
                out_ref, *, block_cols):
    @pl.when(pl.program_id(0) == 0)
    def _():
        out_ref[...] = jnp.zeros(out_ref.shape, jnp.float32)

    masked, target_hit = block_scores(latent_ref, factor_ref, bias_ref, expand_ref, target_ref, block_cols)
    powers = jnp.exp(masked - peak_ref[...])
    score_grad = (powers * scale_ref[...] - jnp.where(target_hit, weight_ref[...], 0.0)).astype(jnp.bfloat16)
    out_ref[...] += lax.dot_general(
        score_grad, factor_ref[...], (((1,), (1,)), ((), ())), preferred_element_type=jnp.float32
    )


def tiles_per_block(tiles, largest):
    for count in (76, 38, 19, 16, 8, 4, 2, 1):
        if count <= largest and tiles % count == 0:
            return count
    return 1


def block_layout(tile_bits, rows, rank, tiles, largest):
    per_block = tiles_per_block(tiles, largest)
    blocks = tiles // per_block
    block_cols = per_block * TILE
    padded = jnp.pad(tile_bits.reshape(rows, blocks, per_block), ((0, 0), (0, 0), (0, TILE - per_block)))
    bits = jnp.where(padded.reshape(rows, blocks * TILE) == 1, 0.0, far_below).astype(jnp.bfloat16)
    expand = (
        lax.broadcasted_iota(jnp.int32, (TILE, block_cols), 0)
        == lax.broadcasted_iota(jnp.int32, (TILE, block_cols), 1) // TILE
    ).astype(jnp.bfloat16)
    specs = [
        pl.BlockSpec((rows, rank), lambda j: (0, 0)),
        pl.BlockSpec((rank, block_cols), lambda j: (0, j)),
        pl.BlockSpec((rows, TILE), lambda j: (0, j)),
        pl.BlockSpec((TILE, block_cols), lambda j: (0, 0)),
        pl.BlockSpec((rows, 1), lambda j: (0, 0)),
    ]
    return blocks, block_cols, bits, expand, specs


def softmax_parts(latent, factor, tile_bits, target_local):
    rows, rank = latent.shape
    width = factor.shape[1]
    tiles = width // TILE
    target = target_local[:, None]
    column_spec = pl.BlockSpec((rows, 1), lambda j: (0, 0))
    params = pltpu.CompilerParams(dimension_semantics=("arbitrary",))
    matmul_flops = 2 * rows * rank * width + 2 * rows * TILE * width
    blocks, block_cols, bits, expand, specs = block_layout(tile_bits, rows, rank, tiles, 76)
    peak, total = pl.pallas_call(
        functools.partial(stats_kernel, block_cols=block_cols),
        grid=(blocks,),
        in_specs=specs,
        out_specs=[column_spec, column_spec],
        out_shape=[jax.ShapeDtypeStruct((rows, 1), jnp.float32)] * 2,
        compiler_params=params,
        cost_estimate=pl.CostEstimate(
            flops=matmul_flops, transcendentals=rows * width, bytes_accessed=rank * width * 2
        ),
    )(latent, factor, bits, expand, target)
    grad_blocks, grad_cols, grad_bits, grad_expand, grad_specs = block_layout(
        tile_bits, rows, rank, tiles, 38
    )

    def grads(peak, scale, weight):
        return pl.pallas_call(
            functools.partial(grad_kernel, block_cols=grad_cols),
            grid=(grad_blocks,),
            in_specs=grad_specs + [column_spec] * 3,
            out_specs=pl.BlockSpec((rows, rank), lambda j: (0, 0)),
            out_shape=jax.ShapeDtypeStruct((rows, rank), jnp.float32),
            compiler_params=params,
            cost_estimate=pl.CostEstimate(
                flops=matmul_flops + 2 * rows * rank * width,
                transcendentals=rows * width,
                bytes_accessed=rank * width * 2,
            ),
        )(latent, factor, grad_bits, grad_expand, target, peak, scale, weight)

    return peak, total, grads


def body(hidden, rank_factor, vocab_factor, lengths, targets, cotangent, grammar, assign):
    row_count = hidden.shape[0]
    rank = rank_factor.shape[0]
    groups = lax.axis_size("dp")
    share = row_count // groups
    width = vocab_factor.shape[1]
    tiles = width // 128
    first = lax.axis_index("vocab") * width
    pair = lax.axis_size("vocab") == 2

    def partner(x):
        return lax.ppermute(x, "vocab", perm=[(0, 1), (1, 0)])

    factor = lax.all_gather(vocab_factor, "dp", axis=0, tiled=True)
    row_words = jnp.repeat(grammar, row_count // grammar.shape[0], axis=0)
    weight = (cotangent.astype(jnp.float32) * lengths.astype(jnp.float32) / PREFIX_MAX)[:, None]

    partial_latent = lax.dot_general(
        hidden, rank_factor, (((1,), (1,)), ((), ())), preferred_element_type=jnp.float32
    )
    latent = lax.psum(partial_latent, "vocab").astype(jnp.bfloat16)
    target_local = targets - first
    shifts = jnp.arange(30, dtype=jnp.int32)
    bits = jnp.right_shift(row_words[:, :, None], shifts) & 1
    tile_bits = bits.reshape(row_count, -1)[:, :tiles]
    local_peak, local_total, grads = softmax_parts(latent, factor, tile_bits, target_local)
    if pair:
        other_peak, other_total = partner(local_peak), partner(local_total)
        peak = jnp.maximum(local_peak, other_peak)
        total = local_total * jnp.exp(local_peak - peak) + other_total * jnp.exp(other_peak - peak)
    else:
        peak = lax.pmax(local_peak, "vocab")
        total = lax.psum(local_total * jnp.exp(local_peak - peak), "vocab")
    rank_partial = grads(peak, weight / total, weight)
    if pair:
        rank_grad = (rank_partial + partner(rank_partial)).astype(jnp.bfloat16)
    else:
        rank_grad = lax.psum(rank_partial, "vocab").astype(jnp.bfloat16)

    grad_factor = lax.psum_scatter(
        lax.dot_general(
            rank_grad, hidden, (((0,), (0,)), ((), ())), preferred_element_type=jnp.float32
        ),
        "dp",
        scatter_dimension=0,
        tiled=True,
    )
    picked = jnp.take(rank_grad, assign, axis=0).reshape(groups, share, rank)
    slot_rank = lax.all_to_all(picked, "dp", split_axis=0, concat_axis=0, tiled=True).reshape(
        row_count, rank
    )
    grad_hidden = jnp.dot(slot_rank, rank_factor, preferred_element_type=jnp.float32).astype(
        jnp.bfloat16
    )
    return (grad_hidden, grad_factor)


def solution(mesh):
    return jax.shard_map(
        body,
        mesh=mesh,
        in_specs=(
            P("dp", "vocab"),
            P(None, "vocab"),
            P("dp", "vocab"),
            P("dp"),
            P("dp"),
            P("dp"),
            P("dp", "vocab"),
            P("dp"),
        ),
        out_specs=(P("dp", "vocab"), P("dp", "vocab")),
        check_vma=False,
    )
```

```python
import jax
import jax.numpy as jnp
from jax import lax
from jax.experimental import pallas as pl
from jax.experimental.pallas import tpu as pltpu
from jax.sharding import PartitionSpec as P
import functools

PREFIX_MAX = 4096


far_below = -1e30
TILE = 128


def block_scores(latent_ref, factor_ref, bias_ref, expand_ref, target_ref, block_cols):
    target_rel = target_ref[...] - pl.program_id(0) * block_cols
    flags = bias_ref[...].astype(jnp.float32)
    rows = flags.shape[0]
    bias = jnp.concatenate(
        [jnp.broadcast_to(flags[:, t : t + 1], (rows, TILE)) for t in range(block_cols // TILE)], axis=1
    )
    logits = jnp.dot(latent_ref[...], factor_ref[...], preferred_element_type=jnp.float32)
    target_hit = lax.broadcasted_iota(jnp.int32, logits.shape, 1) == target_rel
    return jnp.where(target_hit, logits, logits + bias), target_hit


def stats_kernel(latent_ref, factor_ref, bias_ref, expand_ref, target_ref, peak_ref, total_ref, *, block_cols):
    @pl.when(pl.program_id(0) == 0)
    def _():
        peak_ref[...] = jnp.full(peak_ref.shape, far_below, jnp.float32)
        total_ref[...] = jnp.zeros(total_ref.shape, jnp.float32)

    masked, _ = block_scores(latent_ref, factor_ref, bias_ref, expand_ref, target_ref, block_cols)
    old = peak_ref[...]
    new = jnp.maximum(old, jnp.max(masked, axis=1, keepdims=True))
    total_ref[...] = total_ref[...] * jnp.exp(old - new) + jnp.sum(
        jnp.exp(masked - new), axis=1, keepdims=True
    )
    peak_ref[...] = new


def grad_kernel(latent_ref, factor_ref, bias_ref, expand_ref, target_ref, peak_ref, scale_ref, weight_ref,
                out_ref, *, block_cols):
    @pl.when(pl.program_id(0) == 0)
    def _():
        out_ref[...] = jnp.zeros(out_ref.shape, jnp.float32)

    masked, target_hit = block_scores(latent_ref, factor_ref, bias_ref, expand_ref, target_ref, block_cols)
    powers = jnp.exp(masked - peak_ref[...])
    score_grad = (powers * scale_ref[...] - jnp.where(target_hit, weight_ref[...], 0.0)).astype(jnp.bfloat16)
    out_ref[...] += lax.dot_general(
        score_grad, factor_ref[...], (((1,), (1,)), ((), ())), preferred_element_type=jnp.float32
    )


def tiles_per_block(tiles, largest):
    for count in (76, 38, 19, 16, 8, 4, 2, 1):
        if count <= largest and tiles % count == 0:
            return count
    return 1


def block_layout(tile_bits, rows, rank, tiles, largest):
    per_block = tiles_per_block(tiles, largest)
    blocks = tiles // per_block
    block_cols = per_block * TILE
    padded = jnp.pad(tile_bits.reshape(rows, blocks, per_block), ((0, 0), (0, 0), (0, TILE - per_block)))
    bits = jnp.where(padded.reshape(rows, blocks * TILE) == 1, 0.0, far_below).astype(jnp.bfloat16)
    expand = (
        lax.broadcasted_iota(jnp.int32, (TILE, block_cols), 0)
        == lax.broadcasted_iota(jnp.int32, (TILE, block_cols), 1) // TILE
    ).astype(jnp.bfloat16)
    specs = [
        pl.BlockSpec((rows, rank), lambda j: (0, 0)),
        pl.BlockSpec((rank, block_cols), lambda j: (0, j)),
        pl.BlockSpec((rows, TILE), lambda j: (0, j)),
        pl.BlockSpec((TILE, block_cols), lambda j: (0, 0)),
        pl.BlockSpec((rows, 1), lambda j: (0, 0)),
    ]
    return blocks, block_cols, bits, expand, specs


def softmax_parts(latent, factor, tile_bits, target_local):
    rows, rank = latent.shape
    width = factor.shape[1]
    tiles = width // TILE
    target = target_local[:, None]
    column_spec = pl.BlockSpec((rows, 1), lambda j: (0, 0))
    params = pltpu.CompilerParams(dimension_semantics=("arbitrary",))
    matmul_flops = 2 * rows * rank * width + 2 * rows * TILE * width
    blocks, block_cols, bits, expand, specs = block_layout(tile_bits, rows, rank, tiles, 76)
    peak, total = pl.pallas_call(
        functools.partial(stats_kernel, block_cols=block_cols),
        grid=(blocks,),
        in_specs=specs,
        out_specs=[column_spec, column_spec],
        out_shape=[jax.ShapeDtypeStruct((rows, 1), jnp.float32)] * 2,
        compiler_params=params,
        cost_estimate=pl.CostEstimate(
            flops=matmul_flops, transcendentals=rows * width, bytes_accessed=rank * width * 2
        ),
    )(latent, factor, bits, expand, target)
    grad_blocks, grad_cols, grad_bits, grad_expand, grad_specs = block_layout(
        tile_bits, rows, rank, tiles, 38
    )

    def grads(peak, scale, weight):
        return pl.pallas_call(
            functools.partial(grad_kernel, block_cols=grad_cols),
            grid=(grad_blocks,),
            in_specs=grad_specs + [column_spec] * 3,
            out_specs=pl.BlockSpec((rows, rank), lambda j: (0, 0)),
            out_shape=jax.ShapeDtypeStruct((rows, rank), jnp.float32),
            compiler_params=params,
            cost_estimate=pl.CostEstimate(
                flops=matmul_flops + 2 * rows * rank * width,
                transcendentals=rows * width,
                bytes_accessed=rank * width * 2,
            ),
        )(latent, factor, grad_bits, grad_expand, target, peak, scale, weight)

    return peak, total, grads


def body(hidden, rank_factor, vocab_factor, lengths, targets, cotangent, grammar, assign):
    row_count = hidden.shape[0]
    rank = rank_factor.shape[0]
    groups = lax.axis_size("dp")
    share = row_count // groups
    width = vocab_factor.shape[1]
    tiles = width // 128
    first = lax.axis_index("vocab") * width
    pair = lax.axis_size("vocab") == 2

    def partner(x):
        return lax.ppermute(x, "vocab", perm=[(0, 1), (1, 0)])

    factor = lax.all_gather(vocab_factor, "dp", axis=0, tiled=True)
    row_words = jnp.repeat(grammar, row_count // grammar.shape[0], axis=0)
    weight = (cotangent.astype(jnp.float32) * lengths.astype(jnp.float32) / PREFIX_MAX)[:, None]

    partial_latent = lax.dot_general(
        hidden, rank_factor, (((1,), (1,)), ((), ())), preferred_element_type=jnp.float32
    )
    latent = lax.psum(partial_latent, "vocab").astype(jnp.bfloat16)
    target_local = targets - first
    shifts = jnp.arange(30, dtype=jnp.int32)
    bits = jnp.right_shift(row_words[:, :, None], shifts) & 1
    tile_bits = bits.reshape(row_count, -1)[:, :tiles]
    local_peak, local_total, grads = softmax_parts(latent, factor, tile_bits, target_local)
    if pair:
        other_peak, other_total = partner(local_peak), partner(local_total)
        peak = jnp.maximum(local_peak, other_peak)
        total = local_total * jnp.exp(local_peak - peak) + other_total * jnp.exp(other_peak - peak)
    else:
        peak = lax.pmax(local_peak, "vocab")
        total = lax.psum(local_total * jnp.exp(local_peak - peak), "vocab")
    rank_partial = grads(peak, weight / total, weight)
    if pair:
        rank_grad = (rank_partial + partner(rank_partial)).astype(jnp.bfloat16)
    else:
        rank_grad = lax.psum(rank_partial, "vocab").astype(jnp.bfloat16)

    grad_factor = lax.psum_scatter(
        lax.dot_general(
            rank_grad, hidden, (((0,), (0,)), ((), ())), preferred_element_type=jnp.float32
        ),
        "dp",
        scatter_dimension=0,
        tiled=True,
    )
    picked = jnp.take(rank_grad, assign, axis=0).reshape(groups, share, rank)
    slot_rank = lax.all_to_all(picked, "dp", split_axis=0, concat_axis=0, tiled=True).reshape(
        row_count, rank
    )
    grad_hidden = jnp.dot(slot_rank, rank_factor, preferred_element_type=jnp.float32).astype(
        jnp.bfloat16
    )
    return (grad_hidden, grad_factor)


def solution(mesh):
    return jax.shard_map(
        body,
        mesh=mesh,
        in_specs=(
            P("dp", "vocab"),
            P(None, "vocab"),
            P("dp", "vocab"),
            P("dp"),
            P("dp"),
            P("dp"),
            P("dp", "vocab"),
            P("dp"),
        ),
        out_specs=(P("dp", "vocab"), P("dp", "vocab")),
        check_vma=False,
    )
```

```python
import jax
import jax.numpy as jnp
from jax import lax
from jax.experimental import pallas as pl
from jax.experimental.pallas import tpu as pltpu
from jax.sharding import PartitionSpec as P
import functools

PREFIX_MAX = 4096


far_below = -1e30
TILE = 128


def block_scores(latent_ref, factor_ref, bias_ref, target_ref, block_cols):
    target_rel = target_ref[...] - pl.program_id(0) * block_cols
    flags = bias_ref[...].astype(jnp.float32)
    rows = flags.shape[0]
    bias = jnp.concatenate(
        [jnp.broadcast_to(flags[:, t : t + 1], (rows, TILE)) for t in range(block_cols // TILE)], axis=1
    )
    logits = jnp.dot(latent_ref[...], factor_ref[...], preferred_element_type=jnp.float32)
    target_hit = lax.broadcasted_iota(jnp.int32, logits.shape, 1) == target_rel
    return jnp.where(target_hit, logits, logits + bias), target_hit


def stats_kernel(latent_ref, factor_ref, bias_ref, target_ref, peak_ref, total_ref, *, block_cols):
    @pl.when(pl.program_id(0) == 0)
    def _():
        peak_ref[...] = jnp.full(peak_ref.shape, far_below, jnp.float32)
        total_ref[...] = jnp.zeros(total_ref.shape, jnp.float32)

    masked, _ = block_scores(latent_ref, factor_ref, bias_ref, target_ref, block_cols)
    old = peak_ref[...]
    new = jnp.maximum(old, jnp.max(masked, axis=1, keepdims=True))
    total_ref[...] = total_ref[...] * jnp.exp(old - new) + jnp.sum(
        jnp.exp(masked - new), axis=1, keepdims=True
    )
    peak_ref[...] = new


def grad_kernel(latent_ref, factor_ref, bias_ref, target_ref, peak_ref, scale_ref, weight_ref,
                out_ref, *, block_cols):
    @pl.when(pl.program_id(0) == 0)
    def _():
        out_ref[...] = jnp.zeros(out_ref.shape, jnp.float32)

    masked, target_hit = block_scores(latent_ref, factor_ref, bias_ref, target_ref, block_cols)
    powers = jnp.exp(masked - peak_ref[...])
    score_grad = (powers * scale_ref[...] - jnp.where(target_hit, weight_ref[...], 0.0)).astype(jnp.bfloat16)
    out_ref[...] += lax.dot_general(
        score_grad, factor_ref[...], (((1,), (1,)), ((), ())), preferred_element_type=jnp.float32
    )


def tiles_per_block(tiles, largest):
    for count in (76, 38, 19, 16, 8, 4, 2, 1):
        if count <= largest and tiles % count == 0:
            return count
    return 1


def block_layout(tile_bits, rows, rank, tiles, largest):
    per_block = tiles_per_block(tiles, largest)
    blocks = tiles // per_block
    block_cols = per_block * TILE
    padded = jnp.pad(tile_bits.reshape(rows, blocks, per_block), ((0, 0), (0, 0), (0, TILE - per_block)))
    bits = jnp.where(padded.reshape(rows, blocks * TILE) == 1, 0.0, far_below).astype(jnp.bfloat16)
    specs = [
        pl.BlockSpec((rows, rank), lambda j: (0, 0)),
        pl.BlockSpec((rank, block_cols), lambda j: (0, j)),
        pl.BlockSpec((rows, TILE), lambda j: (0, j)),
        pl.BlockSpec((rows, 1), lambda j: (0, 0)),
    ]
    return blocks, block_cols, bits, specs


def softmax_parts(latent, factor, tile_bits, target_local):
    rows, rank = latent.shape
    width = factor.shape[1]
    tiles = width // TILE
    target = target_local[:, None]
    column_spec = pl.BlockSpec((rows, 1), lambda j: (0, 0))
    params = pltpu.CompilerParams(dimension_semantics=("arbitrary",))
    matmul_flops = 2 * rows * rank * width
    blocks, block_cols, bits, specs = block_layout(tile_bits, rows, rank, tiles, 76)
    peak, total = pl.pallas_call(
        functools.partial(stats_kernel, block_cols=block_cols),
        grid=(blocks,),
        in_specs=specs,
        out_specs=[column_spec, column_spec],
        out_shape=[jax.ShapeDtypeStruct((rows, 1), jnp.float32)] * 2,
        compiler_params=params,
        cost_estimate=pl.CostEstimate(
            flops=matmul_flops, transcendentals=rows * width, bytes_accessed=rank * width * 2
        ),
    )(latent, factor, bits, target)
    grad_blocks, grad_cols, grad_bits, grad_specs = block_layout(
        tile_bits, rows, rank, tiles, 38
    )

    def grads(peak, scale, weight):
        return pl.pallas_call(
            functools.partial(grad_kernel, block_cols=grad_cols),
            grid=(grad_blocks,),
            in_specs=grad_specs + [column_spec] * 3,
            out_specs=pl.BlockSpec((rows, rank), lambda j: (0, 0)),
            out_shape=jax.ShapeDtypeStruct((rows, rank), jnp.float32),
            compiler_params=params,
            cost_estimate=pl.CostEstimate(
                flops=matmul_flops + 2 * rows * rank * width,
                transcendentals=rows * width,
                bytes_accessed=rank * width * 2,
            ),
        )(latent, factor, grad_bits, target, peak, scale, weight)

    return peak, total, grads


def body(hidden, rank_factor, vocab_factor, lengths, targets, cotangent, grammar, assign):
    row_count = hidden.shape[0]
    rank = rank_factor.shape[0]
    groups = lax.axis_size("dp")
    share = row_count // groups
    width = vocab_factor.shape[1]
    tiles = width // 128
    first = lax.axis_index("vocab") * width
    pair = lax.axis_size("vocab") == 2

    def partner(x):
        return lax.ppermute(x, "vocab", perm=[(0, 1), (1, 0)])

    factor = lax.all_gather(vocab_factor, "dp", axis=0, tiled=True)
    row_words = jnp.repeat(grammar, row_count // grammar.shape[0], axis=0)
    weight = (cotangent.astype(jnp.float32) * lengths.astype(jnp.float32) / PREFIX_MAX)[:, None]

    partial_latent = lax.dot_general(
        hidden, rank_factor, (((1,), (1,)), ((), ())), preferred_element_type=jnp.float32
    )
    latent = lax.psum(partial_latent, "vocab").astype(jnp.bfloat16)
    target_local = targets - first
    shifts = jnp.arange(30, dtype=jnp.int32)
    bits = jnp.right_shift(row_words[:, :, None], shifts) & 1
    tile_bits = bits.reshape(row_count, -1)[:, :tiles]
    local_peak, local_total, grads = softmax_parts(latent, factor, tile_bits, target_local)
    if pair:
        other_peak, other_total = partner(local_peak), partner(local_total)
        peak = jnp.maximum(local_peak, other_peak)
        total = local_total * jnp.exp(local_peak - peak) + other_total * jnp.exp(other_peak - peak)
    else:
        peak = lax.pmax(local_peak, "vocab")
        total = lax.psum(local_total * jnp.exp(local_peak - peak), "vocab")
    rank_partial = grads(peak, weight / total, weight)
    if pair:
        rank_grad = (rank_partial + partner(rank_partial)).astype(jnp.bfloat16)
    else:
        rank_grad = lax.psum(rank_partial, "vocab").astype(jnp.bfloat16)

    grad_factor = lax.psum_scatter(
        lax.dot_general(
            rank_grad, hidden, (((0,), (0,)), ((), ())), preferred_element_type=jnp.float32
        ),
        "dp",
        scatter_dimension=0,
        tiled=True,
    )
    picked = jnp.take(rank_grad, assign, axis=0).reshape(groups, share, rank)
    slot_rank = lax.all_to_all(picked, "dp", split_axis=0, concat_axis=0, tiled=True).reshape(
        row_count, rank
    )
    grad_hidden = jnp.dot(slot_rank, rank_factor, preferred_element_type=jnp.float32).astype(
        jnp.bfloat16
    )
    return (grad_hidden, grad_factor)


def solution(mesh):
    return jax.shard_map(
        body,
        mesh=mesh,
        in_specs=(
            P("dp", "vocab"),
            P(None, "vocab"),
            P("dp", "vocab"),
            P("dp"),
            P("dp"),
            P("dp"),
            P("dp", "vocab"),
            P("dp"),
        ),
        out_specs=(P("dp", "vocab"), P("dp", "vocab")),
        check_vma=False,
    )
```

```python
import jax
import jax.numpy as jnp
from jax import lax
from jax.experimental import pallas as pl
from jax.experimental.pallas import tpu as pltpu
from jax.sharding import PartitionSpec as P
import functools

PREFIX_MAX = 4096


far_below = -1e30
TILE = 128


def block_scores(latent_ref, factor_ref, bias_ref, target_ref, block_cols):
    target_rel = target_ref[...] - pl.program_id(0) * block_cols
    flags = bias_ref[...].astype(jnp.float32)
    rows = flags.shape[0]
    bias = jnp.concatenate(
        [jnp.broadcast_to(flags[:, t : t + 1], (rows, TILE)) for t in range(block_cols // TILE)], axis=1
    )
    logits = jnp.dot(latent_ref[...], factor_ref[...], preferred_element_type=jnp.float32)
    target_hit = lax.broadcasted_iota(jnp.int32, logits.shape, 1) == target_rel
    return jnp.where(target_hit, logits, logits + bias), target_hit


def stats_kernel(latent_ref, factor_ref, bias_ref, target_ref, peak_ref, total_ref, *, block_cols):
    @pl.when(pl.program_id(0) == 0)
    def _():
        peak_ref[...] = jnp.full(peak_ref.shape, far_below, jnp.float32)
        total_ref[...] = jnp.zeros(total_ref.shape, jnp.float32)

    masked, _ = block_scores(latent_ref, factor_ref, bias_ref, target_ref, block_cols)
    old = peak_ref[...]
    new = jnp.maximum(old, jnp.max(masked, axis=1, keepdims=True))
    total_ref[...] = total_ref[...] * jnp.exp(old - new) + jnp.sum(
        jnp.exp(masked - new), axis=1, keepdims=True
    )
    peak_ref[...] = new


def grad_kernel(latent_ref, factor_ref, bias_ref, target_ref, peak_ref, scale_ref, weight_ref,
                out_ref, *, block_cols):
    @pl.when(pl.program_id(0) == 0)
    def _():
        out_ref[...] = jnp.zeros(out_ref.shape, jnp.float32)

    masked, target_hit = block_scores(latent_ref, factor_ref, bias_ref, target_ref, block_cols)
    powers = jnp.exp(masked - peak_ref[...])
    score_grad = (powers * scale_ref[...] - jnp.where(target_hit, weight_ref[...], 0.0)).astype(jnp.bfloat16)
    out_ref[...] += lax.dot_general(
        score_grad, factor_ref[...], (((1,), (1,)), ((), ())), preferred_element_type=jnp.float32
    )


def tiles_per_block(tiles, largest):
    for count in (76, 38, 19, 16, 8, 4, 2, 1):
        if count <= largest and tiles % count == 0:
            return count
    return 1


def block_layout(tile_bits, rows, rank, tiles, largest):
    per_block = tiles_per_block(tiles, largest)
    blocks = tiles // per_block
    block_cols = per_block * TILE
    padded = jnp.pad(tile_bits.reshape(rows, blocks, per_block), ((0, 0), (0, 0), (0, TILE - per_block)))
    bits = jnp.where(padded.reshape(rows, blocks * TILE) == 1, 0.0, far_below).astype(jnp.bfloat16)
    specs = [
        pl.BlockSpec((rows, rank), lambda j: (0, 0)),
        pl.BlockSpec((rank, block_cols), lambda j: (0, j)),
        pl.BlockSpec((rows, TILE), lambda j: (0, j)),
        pl.BlockSpec((rows, 1), lambda j: (0, 0)),
    ]
    return blocks, block_cols, bits, specs


def softmax_parts(latent, factor, tile_bits, target_local):
    rows, rank = latent.shape
    width = factor.shape[1]
    tiles = width // TILE
    target = target_local[:, None]
    column_spec = pl.BlockSpec((rows, 1), lambda j: (0, 0))
    params = pltpu.CompilerParams(dimension_semantics=("arbitrary",))
    matmul_flops = 2 * rows * rank * width
    blocks, block_cols, bits, specs = block_layout(tile_bits, rows, rank, tiles, 76)
    peak, total = pl.pallas_call(
        functools.partial(stats_kernel, block_cols=block_cols),
        grid=(blocks,),
        in_specs=specs,
        out_specs=[column_spec, column_spec],
        out_shape=[jax.ShapeDtypeStruct((rows, 1), jnp.float32)] * 2,
        compiler_params=params,
        cost_estimate=pl.CostEstimate(
            flops=matmul_flops, transcendentals=rows * width, bytes_accessed=rank * width * 2
        ),
    )(latent, factor, bits, target)
    grad_blocks, grad_cols, grad_bits, grad_specs = block_layout(
        tile_bits, rows, rank, tiles, 76
    )

    def grads(peak, scale, weight):
        return pl.pallas_call(
            functools.partial(grad_kernel, block_cols=grad_cols),
            grid=(grad_blocks,),
            in_specs=grad_specs + [column_spec] * 3,
            out_specs=pl.BlockSpec((rows, rank), lambda j: (0, 0)),
            out_shape=jax.ShapeDtypeStruct((rows, rank), jnp.float32),
            compiler_params=params,
            cost_estimate=pl.CostEstimate(
                flops=matmul_flops + 2 * rows * rank * width,
                transcendentals=rows * width,
                bytes_accessed=rank * width * 2,
            ),
        )(latent, factor, grad_bits, target, peak, scale, weight)

    return peak, total, grads


def body(hidden, rank_factor, vocab_factor, lengths, targets, cotangent, grammar, assign):
    row_count = hidden.shape[0]
    rank = rank_factor.shape[0]
    groups = lax.axis_size("dp")
    share = row_count // groups
    width = vocab_factor.shape[1]
    tiles = width // 128
    first = lax.axis_index("vocab") * width
    pair = lax.axis_size("vocab") == 2

    def partner(x):
        return lax.ppermute(x, "vocab", perm=[(0, 1), (1, 0)])

    factor = lax.all_gather(vocab_factor, "dp", axis=0, tiled=True)
    row_words = jnp.repeat(grammar, row_count // grammar.shape[0], axis=0)
    weight = (cotangent.astype(jnp.float32) * lengths.astype(jnp.float32) / PREFIX_MAX)[:, None]

    partial_latent = lax.dot_general(
        hidden, rank_factor, (((1,), (1,)), ((), ())), preferred_element_type=jnp.float32
    )
    latent = lax.psum(partial_latent, "vocab").astype(jnp.bfloat16)
    target_local = targets - first
    shifts = jnp.arange(30, dtype=jnp.int32)
    bits = jnp.right_shift(row_words[:, :, None], shifts) & 1
    tile_bits = bits.reshape(row_count, -1)[:, :tiles]
    local_peak, local_total, grads = softmax_parts(latent, factor, tile_bits, target_local)
    if pair:
        other_peak, other_total = partner(local_peak), partner(local_total)
        peak = jnp.maximum(local_peak, other_peak)
        total = local_total * jnp.exp(local_peak - peak) + other_total * jnp.exp(other_peak - peak)
    else:
        peak = lax.pmax(local_peak, "vocab")
        total = lax.psum(local_total * jnp.exp(local_peak - peak), "vocab")
    rank_partial = grads(peak, weight / total, weight)
    if pair:
        rank_grad = (rank_partial + partner(rank_partial)).astype(jnp.bfloat16)
    else:
        rank_grad = lax.psum(rank_partial, "vocab").astype(jnp.bfloat16)

    grad_factor = lax.psum_scatter(
        lax.dot_general(
            rank_grad, hidden, (((0,), (0,)), ((), ())), preferred_element_type=jnp.float32
        ),
        "dp",
        scatter_dimension=0,
        tiled=True,
    )
    picked = jnp.take(rank_grad, assign, axis=0).reshape(groups, share, rank)
    slot_rank = lax.all_to_all(picked, "dp", split_axis=0, concat_axis=0, tiled=True).reshape(
        row_count, rank
    )
    grad_hidden = jnp.dot(slot_rank, rank_factor, preferred_element_type=jnp.float32).astype(
        jnp.bfloat16
    )
    return (grad_hidden, grad_factor)


def solution(mesh):
    return jax.shard_map(
        body,
        mesh=mesh,
        in_specs=(
            P("dp", "vocab"),
            P(None, "vocab"),
            P("dp", "vocab"),
            P("dp"),
            P("dp"),
            P("dp"),
            P("dp", "vocab"),
            P("dp"),
        ),
        out_specs=(P("dp", "vocab"), P("dp", "vocab")),
        check_vma=False,
    )
```

```python
import jax
import jax.numpy as jnp
from jax import lax
from jax.experimental import pallas as pl
from jax.experimental.pallas import tpu as pltpu
from jax.sharding import PartitionSpec as P
import functools

PREFIX_MAX = 4096


far_below = -1e30
TILE = 128


def block_scores(latent_ref, factor_ref, bias_ref, target_ref, block_cols):
    target_rel = target_ref[...] - pl.program_id(0) * block_cols
    flags = bias_ref[...].astype(jnp.float32)
    rows = flags.shape[0]
    bias = jnp.concatenate(
        [jnp.broadcast_to(flags[:, t : t + 1], (rows, TILE)) for t in range(block_cols // TILE)], axis=1
    )
    logits = jnp.dot(latent_ref[...], factor_ref[...], preferred_element_type=jnp.float32)
    target_hit = lax.broadcasted_iota(jnp.int32, logits.shape, 1) == target_rel
    return jnp.where(target_hit, logits, logits + bias), target_hit


def stats_kernel(latent_ref, factor_ref, bias_ref, target_ref, peak_ref, total_ref, *, block_cols):
    @pl.when(pl.program_id(0) == 0)
    def _():
        peak_ref[...] = jnp.full(peak_ref.shape, far_below, jnp.float32)
        total_ref[...] = jnp.zeros(total_ref.shape, jnp.float32)

    masked, _ = block_scores(latent_ref, factor_ref, bias_ref, target_ref, block_cols)
    old = peak_ref[...]
    new = jnp.maximum(old, jnp.max(masked, axis=1, keepdims=True))
    total_ref[...] = total_ref[...] * jnp.exp(old - new) + jnp.sum(
        jnp.exp(masked - new), axis=1, keepdims=True
    )
    peak_ref[...] = new


def grad_kernel(latent_ref, factor_ref, bias_ref, target_ref, peak_ref, scale_ref, weight_ref,
                out_ref, *, block_cols):
    @pl.when(pl.program_id(0) == 0)
    def _():
        out_ref[...] = jnp.zeros(out_ref.shape, jnp.float32)

    masked, target_hit = block_scores(latent_ref, factor_ref, bias_ref, target_ref, block_cols)
    powers = jnp.exp(masked - peak_ref[...])
    score_grad = (powers * scale_ref[...] - jnp.where(target_hit, weight_ref[...], 0.0)).astype(jnp.bfloat16)
    out_ref[...] += lax.dot_general(
        score_grad, factor_ref[...], (((1,), (1,)), ((), ())), preferred_element_type=jnp.float32
    )


def tiles_per_block(tiles, largest):
    for count in (76, 38, 19, 16, 8, 4, 2, 1):
        if count <= largest and tiles % count == 0:
            return count
    return 1


def block_layout(tile_bits, rows, rank, tiles, largest):
    per_block = tiles_per_block(tiles, largest)
    blocks = tiles // per_block
    block_cols = per_block * TILE
    padded = jnp.pad(tile_bits.reshape(rows, blocks, per_block), ((0, 0), (0, 0), (0, TILE - per_block)))
    bits = jnp.where(padded.reshape(rows, blocks * TILE) == 1, 0.0, far_below).astype(jnp.bfloat16)
    specs = [
        pl.BlockSpec((rows, rank), lambda j: (0, 0)),
        pl.BlockSpec((rank, block_cols), lambda j: (0, j)),
        pl.BlockSpec((rows, TILE), lambda j: (0, j)),
        pl.BlockSpec((rows, 1), lambda j: (0, 0)),
    ]
    return blocks, block_cols, bits, specs


def softmax_parts(latent, factor, tile_bits, target_local):
    rows, rank = latent.shape
    width = factor.shape[1]
    tiles = width // TILE
    target = target_local[:, None]
    column_spec = pl.BlockSpec((rows, 1), lambda j: (0, 0))
    params = pltpu.CompilerParams(dimension_semantics=("arbitrary",))
    matmul_flops = 2 * rows * rank * width
    blocks, block_cols, bits, specs = block_layout(tile_bits, rows, rank, tiles, 38)
    peak, total = pl.pallas_call(
        functools.partial(stats_kernel, block_cols=block_cols),
        grid=(blocks,),
        in_specs=specs,
        out_specs=[column_spec, column_spec],
        out_shape=[jax.ShapeDtypeStruct((rows, 1), jnp.float32)] * 2,
        compiler_params=params,
        cost_estimate=pl.CostEstimate(
            flops=matmul_flops, transcendentals=rows * width, bytes_accessed=rank * width * 2
        ),
    )(latent, factor, bits, target)
    grad_blocks, grad_cols, grad_bits, grad_specs = block_layout(
        tile_bits, rows, rank, tiles, 38
    )

    def grads(peak, scale, weight):
        return pl.pallas_call(
            functools.partial(grad_kernel, block_cols=grad_cols),
            grid=(grad_blocks,),
            in_specs=grad_specs + [column_spec] * 3,
            out_specs=pl.BlockSpec((rows, rank), lambda j: (0, 0)),
            out_shape=jax.ShapeDtypeStruct((rows, rank), jnp.float32),
            compiler_params=params,
            cost_estimate=pl.CostEstimate(
                flops=matmul_flops + 2 * rows * rank * width,
                transcendentals=rows * width,
                bytes_accessed=rank * width * 2,
            ),
        )(latent, factor, grad_bits, target, peak, scale, weight)

    return peak, total, grads


def body(hidden, rank_factor, vocab_factor, lengths, targets, cotangent, grammar, assign):
    row_count = hidden.shape[0]
    rank = rank_factor.shape[0]
    groups = lax.axis_size("dp")
    share = row_count // groups
    width = vocab_factor.shape[1]
    tiles = width // 128
    first = lax.axis_index("vocab") * width
    pair = lax.axis_size("vocab") == 2

    def partner(x):
        return lax.ppermute(x, "vocab", perm=[(0, 1), (1, 0)])

    factor = lax.all_gather(vocab_factor, "dp", axis=0, tiled=True)
    row_words = jnp.repeat(grammar, row_count // grammar.shape[0], axis=0)
    weight = (cotangent.astype(jnp.float32) * lengths.astype(jnp.float32) / PREFIX_MAX)[:, None]

    partial_latent = lax.dot_general(
        hidden, rank_factor, (((1,), (1,)), ((), ())), preferred_element_type=jnp.float32
    )
    latent = lax.psum(partial_latent, "vocab").astype(jnp.bfloat16)
    target_local = targets - first
    shifts = jnp.arange(30, dtype=jnp.int32)
    bits = jnp.right_shift(row_words[:, :, None], shifts) & 1
    tile_bits = bits.reshape(row_count, -1)[:, :tiles]
    local_peak, local_total, grads = softmax_parts(latent, factor, tile_bits, target_local)
    if pair:
        other_peak, other_total = partner(local_peak), partner(local_total)
        peak = jnp.maximum(local_peak, other_peak)
        total = local_total * jnp.exp(local_peak - peak) + other_total * jnp.exp(other_peak - peak)
    else:
        peak = lax.pmax(local_peak, "vocab")
        total = lax.psum(local_total * jnp.exp(local_peak - peak), "vocab")
    rank_partial = grads(peak, weight / total, weight)
    if pair:
        rank_grad = (rank_partial + partner(rank_partial)).astype(jnp.bfloat16)
    else:
        rank_grad = lax.psum(rank_partial, "vocab").astype(jnp.bfloat16)

    grad_factor = lax.psum_scatter(
        lax.dot_general(
            rank_grad, hidden, (((0,), (0,)), ((), ())), preferred_element_type=jnp.float32
        ),
        "dp",
        scatter_dimension=0,
        tiled=True,
    )
    picked = jnp.take(rank_grad, assign, axis=0).reshape(groups, share, rank)
    slot_rank = lax.all_to_all(picked, "dp", split_axis=0, concat_axis=0, tiled=True).reshape(
        row_count, rank
    )
    grad_hidden = jnp.dot(slot_rank, rank_factor, preferred_element_type=jnp.float32).astype(
        jnp.bfloat16
    )
    return (grad_hidden, grad_factor)


def solution(mesh):
    return jax.shard_map(
        body,
        mesh=mesh,
        in_specs=(
            P("dp", "vocab"),
            P(None, "vocab"),
            P("dp", "vocab"),
            P("dp"),
            P("dp"),
            P("dp"),
            P("dp", "vocab"),
            P("dp"),
        ),
        out_specs=(P("dp", "vocab"), P("dp", "vocab")),
        check_vma=False,
    )
```

```python
import jax
import jax.numpy as jnp
from jax import lax
from jax.experimental import pallas as pl
from jax.experimental.pallas import tpu as pltpu
from jax.sharding import PartitionSpec as P
import functools

PREFIX_MAX = 4096


far_below = -1e30
TILE = 128


def block_scores(latent_ref, factor_ref, bias_ref, target_ref, block_cols):
    target_rel = target_ref[...] - pl.program_id(0) * block_cols
    flags = bias_ref[...].astype(jnp.float32)
    rows = flags.shape[0]
    bias = jnp.concatenate(
        [jnp.broadcast_to(flags[:, t : t + 1], (rows, TILE)) for t in range(block_cols // TILE)], axis=1
    )
    logits = jnp.dot(latent_ref[...], factor_ref[...], preferred_element_type=jnp.float32)
    target_hit = lax.broadcasted_iota(jnp.int32, logits.shape, 1) == target_rel
    return jnp.where(target_hit, logits, logits + bias), target_hit


def stats_kernel(latent_ref, factor_ref, bias_ref, target_ref, peak_ref, total_ref, *, block_cols):
    @pl.when(pl.program_id(0) == 0)
    def _():
        peak_ref[...] = jnp.full(peak_ref.shape, far_below, jnp.float32)
        total_ref[...] = jnp.zeros(total_ref.shape, jnp.float32)

    masked, _ = block_scores(latent_ref, factor_ref, bias_ref, target_ref, block_cols)
    old = peak_ref[...]
    new = jnp.maximum(old, jnp.max(masked, axis=1, keepdims=True))
    total_ref[...] = total_ref[...] * jnp.exp(old - new) + jnp.sum(
        jnp.exp(masked - new), axis=1, keepdims=True
    )
    peak_ref[...] = new


def grad_kernel(latent_ref, factor_ref, bias_ref, target_ref, peak_ref, scale_ref, weight_ref,
                out_ref, *, block_cols):
    @pl.when(pl.program_id(0) == 0)
    def _():
        out_ref[...] = jnp.zeros(out_ref.shape, jnp.float32)

    masked, target_hit = block_scores(latent_ref, factor_ref, bias_ref, target_ref, block_cols)
    powers = jnp.exp(masked - peak_ref[...])
    score_grad = (powers * scale_ref[...] - jnp.where(target_hit, weight_ref[...], 0.0)).astype(jnp.bfloat16)
    out_ref[...] += lax.dot_general(
        score_grad, factor_ref[...], (((1,), (1,)), ((), ())), preferred_element_type=jnp.float32
    )


def tiles_per_block(tiles, largest):
    for count in (76, 38, 19, 16, 8, 4, 2, 1):
        if count <= largest and tiles % count == 0:
            return count
    return 1


def block_layout(tile_bits, rows, rank, tiles, largest):
    per_block = tiles_per_block(tiles, largest)
    blocks = tiles // per_block
    block_cols = per_block * TILE
    padded = jnp.pad(tile_bits.reshape(rows, blocks, per_block), ((0, 0), (0, 0), (0, TILE - per_block)))
    bits = jnp.where(padded.reshape(rows, blocks * TILE) == 1, 0.0, far_below).astype(jnp.bfloat16)
    specs = [
        pl.BlockSpec((rows, rank), lambda j: (0, 0)),
        pl.BlockSpec((rank, block_cols), lambda j: (0, j)),
        pl.BlockSpec((rows, TILE), lambda j: (0, j)),
        pl.BlockSpec((rows, 1), lambda j: (0, 0)),
    ]
    return blocks, block_cols, bits, specs


def softmax_parts(latent, factor, tile_bits, target_local):
    rows, rank = latent.shape
    width = factor.shape[1]
    tiles = width // TILE
    target = target_local[:, None]
    column_spec = pl.BlockSpec((rows, 1), lambda j: (0, 0))
    params = pltpu.CompilerParams(dimension_semantics=("arbitrary",))
    matmul_flops = 2 * rows * rank * width
    blocks, block_cols, bits, specs = block_layout(tile_bits, rows, rank, tiles, 76)
    peak, total = pl.pallas_call(
        functools.partial(stats_kernel, block_cols=block_cols),
        grid=(blocks,),
        in_specs=specs,
        out_specs=[column_spec, column_spec],
        out_shape=[jax.ShapeDtypeStruct((rows, 1), jnp.float32)] * 2,
        compiler_params=params,
        cost_estimate=pl.CostEstimate(
            flops=matmul_flops, transcendentals=rows * width, bytes_accessed=rank * width * 2
        ),
    )(latent, factor, bits, target)
    grad_blocks, grad_cols, grad_bits, grad_specs = block_layout(
        tile_bits, rows, rank, tiles, 19
    )

    def grads(peak, scale, weight):
        return pl.pallas_call(
            functools.partial(grad_kernel, block_cols=grad_cols),
            grid=(grad_blocks,),
            in_specs=grad_specs + [column_spec] * 3,
            out_specs=pl.BlockSpec((rows, rank), lambda j: (0, 0)),
            out_shape=jax.ShapeDtypeStruct((rows, rank), jnp.float32),
            compiler_params=params,
            cost_estimate=pl.CostEstimate(
                flops=matmul_flops + 2 * rows * rank * width,
                transcendentals=rows * width,
                bytes_accessed=rank * width * 2,
            ),
        )(latent, factor, grad_bits, target, peak, scale, weight)

    return peak, total, grads


def body(hidden, rank_factor, vocab_factor, lengths, targets, cotangent, grammar, assign):
    row_count = hidden.shape[0]
    rank = rank_factor.shape[0]
    groups = lax.axis_size("dp")
    share = row_count // groups
    width = vocab_factor.shape[1]
    tiles = width // 128
    first = lax.axis_index("vocab") * width
    pair = lax.axis_size("vocab") == 2

    def partner(x):
        return lax.ppermute(x, "vocab", perm=[(0, 1), (1, 0)])

    factor = lax.all_gather(vocab_factor, "dp", axis=0, tiled=True)
    row_words = jnp.repeat(grammar, row_count // grammar.shape[0], axis=0)
    weight = (cotangent.astype(jnp.float32) * lengths.astype(jnp.float32) / PREFIX_MAX)[:, None]

    partial_latent = lax.dot_general(
        hidden, rank_factor, (((1,), (1,)), ((), ())), preferred_element_type=jnp.float32
    )
    latent = lax.psum(partial_latent, "vocab").astype(jnp.bfloat16)
    target_local = targets - first
    shifts = jnp.arange(30, dtype=jnp.int32)
    bits = jnp.right_shift(row_words[:, :, None], shifts) & 1
    tile_bits = bits.reshape(row_count, -1)[:, :tiles]
    local_peak, local_total, grads = softmax_parts(latent, factor, tile_bits, target_local)
    if pair:
        other_peak, other_total = partner(local_peak), partner(local_total)
        peak = jnp.maximum(local_peak, other_peak)
        total = local_total * jnp.exp(local_peak - peak) + other_total * jnp.exp(other_peak - peak)
    else:
        peak = lax.pmax(local_peak, "vocab")
        total = lax.psum(local_total * jnp.exp(local_peak - peak), "vocab")
    rank_partial = grads(peak, weight / total, weight)
    if pair:
        rank_grad = (rank_partial + partner(rank_partial)).astype(jnp.bfloat16)
    else:
        rank_grad = lax.psum(rank_partial, "vocab").astype(jnp.bfloat16)

    grad_factor = lax.psum_scatter(
        lax.dot_general(
            rank_grad, hidden, (((0,), (0,)), ((), ())), preferred_element_type=jnp.float32
        ),
        "dp",
        scatter_dimension=0,
        tiled=True,
    )
    picked = jnp.take(rank_grad, assign, axis=0).reshape(groups, share, rank)
    slot_rank = lax.all_to_all(picked, "dp", split_axis=0, concat_axis=0, tiled=True).reshape(
        row_count, rank
    )
    grad_hidden = jnp.dot(slot_rank, rank_factor, preferred_element_type=jnp.float32).astype(
        jnp.bfloat16
    )
    return (grad_hidden, grad_factor)


def solution(mesh):
    return jax.shard_map(
        body,
        mesh=mesh,
        in_specs=(
            P("dp", "vocab"),
            P(None, "vocab"),
            P("dp", "vocab"),
            P("dp"),
            P("dp"),
            P("dp"),
            P("dp", "vocab"),
            P("dp"),
        ),
        out_specs=(P("dp", "vocab"), P("dp", "vocab")),
        check_vma=False,
    )
```
